32 devices in a mesh: row: 8 (over z, y), rep: 4 (over x, core).
Axes of the slice: x: 2, y: 2, z: 4, core: 2. Of those that a mesh axis runs over, the one named last changes fastest.
Arguments:
- features: bfloat16 [2048, 256], P('row'), may hold values from -6 to 6
- cotangent: bfloat16 [2048, 256], P('row'), may hold values from -0.3125 to 0.3125
- weight_one: bfloat16 [256, 256], replicated, may hold values from -0.375 to 0.375
- weight_two: bfloat16 [256, 256], replicated, may hold values from -0.375 to 0.375
- block_index: int32 [8, 4, 2, 4], P('row', 'rep'), may hold values from 0 to 15, as said below
- block_count: int32 [8, 4, 2], P('row', 'rep'), may hold values from 0 to 4
- block_values: bfloat16 [8, 4, 2, 4, 128, 128], P('row', 'rep'), as said below
Outputs:
- logits: bfloat16 [2048, 256], P(('row', 'rep'))
- grad_one: float32 [256, 256], replicated
- grad_two: float32 [256, 256], replicated
The draws below stay inside these ranges and needn't reach their ends.
Inputs may be any that keep to these rules, and one draw needn't show every extreme that they name: block_index[i, j, a, s] lies in [j * 4, (j + 1) * 4); for s < block_count[i, j, a] the entries rise strictly; later entries equal j * 4 and are not part of A. `block_values`: A is symmetric: block (r, c) is listed exactly when block (c, r) is, and its entries are the transpose of those of block (c, r). Entries are normal with standard deviation (0.5 * 128 * 16) ** -0.5, cut at five such deviations; blocks on the diagonal are symmetric.
All inputs are finite; a program needn't handle non-finite values.
Results may differ from the reference program's by a relative error of at most 0.0059.
Values may be sent and summed in bfloat16 or wider, within the bound.
No kernel may reach another device: no remote copies, remote signals or barrier semaphores. Data moves between devices by JAX's collectives and lax.ppermute only.
A program may use at most 64 MiB of HBM per device.

```python
import math
import jax
import jax.numpy as jnp
from jax import lax

F = 256
BLK = 128
BR = 2
SHARDS = 8
COPIES = 4
SPR = 4
NB = 16
NODES = 2048


def layout(key):
    density = jax.random.randint(jax.random.fold_in(key, 1), (SHARDS,), 1, 9)
    noise = jax.random.randint(jax.random.fold_in(key, 2), (NB, NB), 0, 16)
    row_ids = jnp.arange(NB, dtype=jnp.int32)[:, None]
    col_ids = jnp.arange(NB, dtype=jnp.int32)[None, :]
    paired = jnp.where(row_ids <= col_ids, noise, noise.T)
    row_shard = row_ids // BR
    col_shard = col_ids // BR
    level = density[row_shard] + density[col_shard]
    near_band = jnp.abs(row_ids - col_ids) <= 1
    full_shard = jax.random.randint(jax.random.fold_in(key, 3), (), 0, SHARDS)
    full_group = jax.random.randint(jax.random.fold_in(key, 4), (), 0, COPIES)
    forced = (row_shard == full_shard) & (col_ids // SPR == full_group) | (col_shard == full_shard) & (row_ids // SPR == full_group)
    present = ((paired < level) | near_band | forced).astype(jnp.int32)
    region = present.reshape(SHARDS, BR, COPIES, SPR).transpose(0, 2, 1, 3)
    position = jnp.arange(SPR, dtype=jnp.int32)
    score = (1 - region) * SPR + position
    order = jnp.argsort(score, axis=-1, stable=True).astype(jnp.int32)
    counts = jnp.sum(region, axis=-1).astype(jnp.int32)
    live_slots = position < counts[..., None]
    group_base = (jnp.arange(COPIES, dtype=jnp.int32) * SPR)[None, :, None, None]
    columns = jnp.where(live_slots, order, 0) + group_base
    return (columns, counts)


def draw_block_index(key, part):
    return layout(key)[0]


def draw_block_count(key, part):
    return layout(key)[1]


def draw_block_values(key, part):
    columns, counts = layout(key)
    row_base = (jnp.arange(SHARDS, dtype=jnp.int32) * BR)[:, None, None, None] + jnp.arange(BR, dtype=jnp.int32)[None, None, :, None]
    block_rows = jnp.broadcast_to(row_base, columns.shape)
    value_key = jax.random.fold_in(key, 7)
    factor = (0.5 * BLK * NB) ** (-0.5)

    def one_block(row_index, column_index):
        low_index = jnp.minimum(row_index, column_index)
        high_index = jnp.maximum(row_index, column_index)
        base_block = jnp.clip(jax.random.normal(jax.random.fold_in(value_key, low_index * NB + high_index), (BLK, BLK), jnp.float32), -5.0, 5.0)
        twin_block = jnp.clip((base_block + base_block.T) * math.sqrt(0.5), -5.0, 5.0)
        chosen = jnp.where(row_index == column_index, twin_block, jnp.where(row_index < column_index, base_block, base_block.T))
        return chosen * factor

    def one_shard(inputs):
        shard_rows, shard_columns = inputs
        flat = jax.vmap(one_block)(shard_rows.reshape(-1), shard_columns.reshape(-1))
        return flat.reshape(COPIES, BR, SPR, BLK, BLK).astype(jnp.bfloat16)
    return lax.map(one_shard, (block_rows, columns))


def block_scale(rng, extent, split, smallest, high):
    gain, own = 1.0, jax.random.fold_in(rng, 6)
    for dim, blocks in split:
        draws = jnp.exp(jax.random.uniform(jax.random.fold_in(own, dim), (blocks,), jnp.float32, smallest / len(split), high / len(split)))
        gain = gain * jnp.repeat(draws, extent[dim] // blocks).reshape([-1 if axis == dim else 1 for axis in range(len(extent))])
    return gain


def scatter_about(rng, dims, deviation, most, cuts=(), kind=jnp.bfloat16):
    loudness = block_scale(rng, dims, cuts, -0.22, 0.18) if cuts else 1.0
    entries = jax.random.normal(rng, dims, jnp.float32) * deviation * loudness
    return jnp.minimum(jnp.maximum(entries, -most), most).astype(kind)


def setup_inputs(seed: int = 0) -> dict:
    key_of = jax.random.split(jax.random.key(seed), 8)
    features = scatter_about(key_of[0], (NODES, F), 1.0, 6.0, ((0, 8),))
    cotangent = scatter_about(key_of[1], (NODES, F), (NODES ** -0.5), 0.3125, ((0, 8),))
    weight_one = scatter_about(key_of[2], (F, F), F ** -0.5, 0.375)
    weight_two = scatter_about(key_of[3], (F, F), F ** -0.5, 0.375)
    block_index = draw_block_index(jax.random.fold_in(key_of[7], 71), 0)
    block_count = draw_block_count(jax.random.fold_in(key_of[7], 71), 0)
    block_values = draw_block_values(jax.random.fold_in(key_of[7], 71), 0)
    return {"features": features, "cotangent": cotangent, "weight_one": weight_one, "weight_two": weight_two, "block_index": block_index, "block_count": block_count, "block_values": block_values}


def aggregate(source, block_index, block_count, block_values):
    blocks = source.reshape(NB, BLK, F)
    position = jnp.arange(SPR, dtype=jnp.int32)

    def one_shard(inputs):
        columns, counts, values = inputs
        picked = blocks[columns].astype(jnp.float32)
        live_slots = position[None, None, :] < counts[:, :, None]
        picked = jnp.where(live_slots[:, :, :, None, None], picked, 0.0)
        total = jnp.einsum("crsab,crsbf->raf", values.astype(jnp.float32), picked)
        return total.reshape(BR * BLK, F)

    result = lax.map(one_shard, (block_index, block_count, block_values))
    return result.reshape(NODES, F)


def reference(features, cotangent, weight_one, weight_two, block_index, block_count, block_values):
    agg_one = aggregate(features, block_index, block_count, block_values).astype(jnp.bfloat16)
    pre_one = jnp.dot(agg_one, weight_one, preferred_element_type=jnp.float32)
    hidden = jax.nn.silu(pre_one).astype(jnp.bfloat16)
    agg_two = aggregate(hidden, block_index, block_count, block_values).astype(jnp.bfloat16)
    logits = jnp.dot(agg_two, weight_two, preferred_element_type=jnp.float32).astype(jnp.bfloat16)
    grad_two = jnp.dot(agg_two.T, cotangent, preferred_element_type=jnp.float32)
    back_signal = jnp.dot(cotangent, weight_two.T, preferred_element_type=jnp.float32).astype(jnp.bfloat16)
    carried = aggregate(back_signal, block_index, block_count, block_values)
    gate_value = jax.nn.sigmoid(pre_one)
    pre_grad = (carried * (gate_value + pre_one * gate_value * (1.0 - gate_value))).astype(jnp.bfloat16)
    grad_one = jnp.dot(agg_one.T, pre_grad, preferred_element_type=jnp.float32)
    return (logits, grad_one, grad_two)
```

```python
import jax
import jax.numpy as jnp
from jax import lax
from jax.sharding import PartitionSpec as P

AXES = ("row", "rep")


def is_pow2(n):
    return n > 0 and (n & (n - 1)) == 0


def bit_pairs(devices, bit):
    return [(d, d ^ (1 << bit)) for d in range(devices)]


def reduce_scatter_bits(y, me, bits, devices):
    for step, bit in enumerate(bits):
        axis = len(bits) - 1 - step
        mine = (me >> bit) & 1
        keep = lax.dynamic_index_in_dim(y, mine, axis, keepdims=False)
        send = lax.dynamic_index_in_dim(y, 1 - mine, axis, keepdims=False)
        y = keep + lax.ppermute(send, AXES, bit_pairs(devices, bit))
    return y


def all_gather_bits(z, me, bits, devices):
    for step, bit in enumerate(reversed(bits)):
        mine = (me >> bit) & 1
        other = lax.ppermute(z, AXES, bit_pairs(devices, bit))
        low = jnp.where(mine == 0, z, other)
        high = jnp.where(mine == 0, other, z)
        z = jnp.stack([low, high], axis=step)
    return z


def gather_rounds(x, rows, copies):
    sections = rows // copies
    pieces = []
    for t in range(sections):
        pairs = []
        for r in range(rows):
            for c in range(copies):
                q = c * sections + (r + t) % sections
                pairs.append((q * copies + r // sections, r * copies + c))
        pieces.append(lax.ppermute(x, AXES, pairs))
    return jnp.stack(pieces)


def local_product(pieces, block_index, block_count, block_values, row_index, copy_index):
    sections = pieces.shape[0]
    block_rows = block_values.shape[2]
    slot_count = block_values.shape[3]
    block_side = block_values.shape[-1]
    width = pieces.shape[-1]
    panels = pieces.reshape(sections * block_rows, block_side, width)
    local = block_index[0, 0] - copy_index * slot_count
    shard = local // block_rows
    arrival = (shard - row_index) % sections
    columns = arrival * block_rows + local % block_rows
    live_slots = jnp.arange(slot_count, dtype=jnp.int32)[None, :] < block_count[0, 0][:, None]
    picked = jnp.take(panels, columns.reshape(-1), axis=0).reshape(
        block_rows, slot_count, block_side, width
    )
    picked = jnp.where(live_slots[:, :, None, None], picked, jnp.zeros((), picked.dtype))
    partial_value = lax.dot_general(
        block_values[0, 0],
        picked,
        (((1, 3), (1, 2)), ((0,), (0,))),
        preferred_element_type=jnp.float32,
    )
    return partial_value.reshape(block_rows * block_side, width)


def shards(features, cotangent, weight_one, weight_two, block_index, block_count, block_values):
    rows = lax.axis_size("row")
    copies = lax.axis_size("rep")
    row_index = lax.axis_index("row")
    copy_index = lax.axis_index("rep")
    devices = rows * copies
    me = row_index * copies + copy_index
    node_rows, feature_width = features.shape
    share_rows = node_rows // copies
    rep_levels = copies.bit_length() - 1
    rep_bits = list(range(rep_levels))
    all_bits = list(range(devices.bit_length() - 1))

    def reduce_rep(partial_value):
        y = partial_value.reshape([2] * rep_levels + [share_rows, partial_value.shape[-1]])
        return reduce_scatter_bits(y, me, rep_bits, devices)

    def gather_rep(z):
        return all_gather_bits(z, me, rep_bits, devices).reshape(node_rows, z.shape[-1])

    back_signal = lax.dot_general(
        cotangent, weight_two, (((1,), (1,)), ((), ())), preferred_element_type=jnp.float32
    ).astype(jnp.bfloat16)
    stage_in = jnp.concatenate([features, back_signal], axis=1)
    pieces = gather_rounds(stage_in, rows, copies)
    both = reduce_rep(
        local_product(pieces, block_index, block_count, block_values, row_index, copy_index)
    )
    agg_one = both[:, :feature_width].astype(jnp.bfloat16)
    carried = both[:, feature_width:]
    pre_one = jnp.dot(agg_one, weight_one, preferred_element_type=jnp.float32)
    hidden = jax.nn.silu(pre_one).astype(jnp.bfloat16)
    gate_value = jax.nn.sigmoid(pre_one)
    pre_grad = (carried * (gate_value + pre_one * gate_value * (1.0 - gate_value))).astype(
        jnp.bfloat16
    )
    grad_one = lax.dot_general(
        agg_one, pre_grad, (((0,), (0,)), ((), ())), preferred_element_type=jnp.float32
    )

    hidden_full = gather_rep(hidden)
    pieces_two = gather_rounds(hidden_full, rows, copies)
    agg_two = reduce_rep(
        local_product(pieces_two, block_index, block_count, block_values, row_index, copy_index)
    ).astype(jnp.bfloat16)
    logits = jnp.dot(agg_two, weight_two, preferred_element_type=jnp.float32).astype(jnp.bfloat16)
    cotangent_own = lax.dynamic_slice_in_dim(cotangent, copy_index * share_rows, share_rows, 0)
    grad_two = lax.dot_general(
        agg_two, cotangent_own, (((0,), (0,)), ((), ())), preferred_element_type=jnp.float32
    )

    grads = jnp.stack([grad_one, grad_two])
    total = grads.size
    levels = len(all_bits)
    segment = grads.reshape([2] * levels + [total // devices])
    summed = reduce_scatter_bits(segment, me, all_bits, devices)
    grads = all_gather_bits(summed, me, all_bits, devices).reshape(grads.shape)
    return (logits, grads[0], grads[1])


def solution(mesh):
    rows = mesh.shape["row"]
    copies = mesh.shape["rep"]
    if not (is_pow2(rows) and is_pow2(copies) and rows % copies == 0):
        raise ValueError("unsupported mesh")
    in_specs = (
        P("row", None),
        P("row", None),
        P(),
        P(),
        P("row", "rep", None, None),
        P("row", "rep", None),
        P("row", "rep", None, None, None, None),
    )
    out_specs = (P(("row", "rep"), None), P(), P())
    return jax.shard_map(shards, mesh=mesh, in_specs=in_specs, out_specs=out_specs, check_vma=False)
```

```python
import jax
import jax.numpy as jnp
from jax import lax
from jax.sharding import PartitionSpec as P

AXES = ("row", "rep")


def is_pow2(n):
    return n > 0 and (n & (n - 1)) == 0


def bit_pairs(devices, bit):
    return [(d, d ^ (1 << bit)) for d in range(devices)]


def reduce_scatter_bits(y, me, bits, devices):
    for step, bit in enumerate(bits):
        axis = len(bits) - 1 - step
        mine = (me >> bit) & 1
        keep = lax.dynamic_index_in_dim(y, mine, axis, keepdims=False)
        send = lax.dynamic_index_in_dim(y, 1 - mine, axis, keepdims=False)
        y = keep + lax.ppermute(send, AXES, bit_pairs(devices, bit))
    return y


def all_gather_bits(z, me, bits, devices):
    for step, bit in enumerate(reversed(bits)):
        mine = (me >> bit) & 1
        other = lax.ppermute(z, AXES, bit_pairs(devices, bit))
        low = jnp.where(mine == 0, z, other)
        high = jnp.where(mine == 0, other, z)
        z = jnp.stack([low, high], axis=step)
    return z


def gather_rounds(x, rows, copies):
    sections = rows // copies
    pieces = []
    for t in range(sections):
        pairs = []
        for r in range(rows):
            for c in range(copies):
                q = c * sections + (r + t) % sections
                pairs.append((q * copies + r // sections, r * copies + c))
        pieces.append(lax.ppermute(x, AXES, pairs))
    return jnp.stack(pieces)


def local_product(pieces, block_index, block_count, block_values, row_index, copy_index):
    sections = pieces.shape[0]
    block_rows = block_values.shape[2]
    slot_count = block_values.shape[3]
    block_side = block_values.shape[-1]
    width = pieces.shape[-1]
    panels = pieces.reshape(sections * block_rows, block_side, width)
    local = block_index[0, 0] - copy_index * slot_count
    shard = local // block_rows
    arrival = (shard - row_index) % sections
    columns = arrival * block_rows + local % block_rows
    live_slots = jnp.arange(slot_count, dtype=jnp.int32)[None, :] < block_count[0, 0][:, None]
    picked = jnp.take(panels, columns.reshape(-1), axis=0).reshape(
        block_rows, slot_count, block_side, width
    )
    picked = jnp.where(live_slots[:, :, None, None], picked, jnp.zeros((), picked.dtype))
    partial_value = lax.dot_general(
        block_values[0, 0],
        picked,
        (((1, 3), (1, 2)), ((0,), (0,))),
        preferred_element_type=jnp.float32,
    )
    return partial_value.reshape(block_rows * block_side, width)


def shards(features, cotangent, weight_one, weight_two, block_index, block_count, block_values):
    rows = lax.axis_size("row")
    copies = lax.axis_size("rep")
    row_index = lax.axis_index("row")
    copy_index = lax.axis_index("rep")
    devices = rows * copies
    me = row_index * copies + copy_index
    node_rows, feature_width = features.shape
    share_rows = node_rows // copies
    rep_levels = copies.bit_length() - 1
    rep_bits = list(range(rep_levels))
    all_bits = list(range(devices.bit_length() - 1))

    def reduce_rep(partial_value):
        y = partial_value.reshape([2] * rep_levels + [share_rows, partial_value.shape[-1]])
        return reduce_scatter_bits(y, me, rep_bits, devices)

    def gather_rep(z):
        return all_gather_bits(z, me, rep_bits, devices).reshape(node_rows, z.shape[-1])

    back_signal = lax.dot_general(
        cotangent, weight_two, (((1,), (1,)), ((), ())), preferred_element_type=jnp.float32
    ).astype(jnp.bfloat16)
    stage_in = jnp.concatenate([features, back_signal, cotangent], axis=1)
    pieces = gather_rounds(stage_in, rows, copies)
    both = reduce_rep(
        local_product(pieces, block_index, block_count, block_values, row_index, copy_index)
    )
    agg_one = both[:, :feature_width].astype(jnp.bfloat16)
    carried = both[:, feature_width : 2 * feature_width]
    spread_cotangent = both[:, 2 * feature_width :]
    pre_one = jnp.dot(agg_one, weight_one, preferred_element_type=jnp.float32)
    hidden = jax.nn.silu(pre_one).astype(jnp.bfloat16)
    gate_value = jax.nn.sigmoid(pre_one)
    pre_grad = (carried * (gate_value + pre_one * gate_value * (1.0 - gate_value))).astype(
        jnp.bfloat16
    )
    grad_one = lax.dot_general(
        agg_one, pre_grad, (((0,), (0,)), ((), ())), preferred_element_type=jnp.float32
    )
    grad_two = lax.dot_general(
        hidden.astype(jnp.float32),
        spread_cotangent,
        (((0,), (0,)), ((), ())),
        precision=lax.Precision.HIGHEST,
        preferred_element_type=jnp.float32,
    )
    grads = jnp.stack([grad_one, grad_two])
    total = grads.size
    levels = len(all_bits)
    segment = grads.reshape([2] * levels + [total // devices])
    summed = reduce_scatter_bits(segment, me, all_bits, devices)
    grads = all_gather_bits(summed, me, all_bits, devices).reshape(grads.shape)

    hidden_full = gather_rep(hidden)
    pieces_two = gather_rounds(hidden_full, rows, copies)
    agg_two = reduce_rep(
        local_product(pieces_two, block_index, block_count, block_values, row_index, copy_index)
    ).astype(jnp.bfloat16)
    logits = jnp.dot(agg_two, weight_two, preferred_element_type=jnp.float32).astype(jnp.bfloat16)
    return (logits, grads[0], grads[1])


def solution(mesh):
    rows = mesh.shape["row"]
    copies = mesh.shape["rep"]
    if not (is_pow2(rows) and is_pow2(copies) and rows % copies == 0):
        raise ValueError("unsupported mesh")
    in_specs = (
        P("row", None),
        P("row", None),
        P(),
        P(),
        P("row", "rep", None, None),
        P("row", "rep", None),
        P("row", "rep", None, None, None, None),
    )
    out_specs = (P(("row", "rep"), None), P(), P())
    return jax.shard_map(shards, mesh=mesh, in_specs=in_specs, out_specs=out_specs, check_vma=False)
```

```python
import jax
import jax.numpy as jnp
from jax import lax
from jax.sharding import PartitionSpec as P

AXES = ("row", "rep")


def is_pow2(n):
    return n > 0 and (n & (n - 1)) == 0


def bit_pairs(devices, bit):
    return [(d, d ^ (1 << bit)) for d in range(devices)]


def reduce_scatter_bits(y, me, bits, devices):
    for step, bit in enumerate(bits):
        axis = len(bits) - 1 - step
        mine = (me >> bit) & 1
        keep = lax.dynamic_index_in_dim(y, mine, axis, keepdims=False)
        send = lax.dynamic_index_in_dim(y, 1 - mine, axis, keepdims=False)
        y = keep + lax.ppermute(send, AXES, bit_pairs(devices, bit))
    return y


def all_gather_bits(z, me, bits, devices):
    for step, bit in enumerate(reversed(bits)):
        mine = (me >> bit) & 1
        other = lax.ppermute(z, AXES, bit_pairs(devices, bit))
        low = jnp.where(mine == 0, z, other)
        high = jnp.where(mine == 0, other, z)
        z = jnp.stack([low, high], axis=step)
    return z


def gather_rounds(x, rows, copies):
    sections = rows // copies
    pieces = []
    for t in range(sections):
        pairs = []
        for r in range(rows):
            for c in range(copies):
                q = c * sections + (r + t) % sections
                pairs.append((q * copies + r // sections, r * copies + c))
        pieces.append(lax.ppermute(x, AXES, pairs))
    return jnp.stack(pieces)


def local_product(pieces, block_index, block_count, block_values, row_index, copy_index):
    sections = pieces.shape[0]
    block_rows = block_values.shape[2]
    slot_count = block_values.shape[3]
    block_side = block_values.shape[-1]
    width = pieces.shape[-1]
    panels = pieces.reshape(sections * block_rows, block_side, width)
    local = block_index[0, 0] - copy_index * slot_count
    shard = local // block_rows
    arrival = (shard - row_index) % sections
    columns = arrival * block_rows + local % block_rows
    live_slots = jnp.arange(slot_count, dtype=jnp.int32)[None, :] < block_count[0, 0][:, None]
    picked = jnp.take(panels, columns.reshape(-1), axis=0).reshape(
        block_rows, slot_count, block_side, width
    )
    picked = jnp.where(live_slots[:, :, None, None], picked, jnp.zeros((), picked.dtype))
    partial_value = lax.dot_general(
        block_values[0, 0],
        picked,
        (((1, 3), (1, 2)), ((0,), (0,))),
        preferred_element_type=jnp.float32,
    )
    return partial_value.reshape(block_rows * block_side, width)


def shards(features, cotangent, weight_one, weight_two, block_index, block_count, block_values):
    rows = lax.axis_size("row")
    copies = lax.axis_size("rep")
    row_index = lax.axis_index("row")
    copy_index = lax.axis_index("rep")
    devices = rows * copies
    me = row_index * copies + copy_index
    node_rows, feature_width = features.shape
    share_rows = node_rows // copies
    rep_levels = copies.bit_length() - 1
    rep_bits = list(range(rep_levels))
    all_bits = list(range(devices.bit_length() - 1))

    def reduce_rep(partial_value):
        y = partial_value.reshape([2] * rep_levels + [share_rows, partial_value.shape[-1]])
        return reduce_scatter_bits(y, me, rep_bits, devices)

    def gather_rep(z):
        return all_gather_bits(z, me, rep_bits, devices).reshape(node_rows, z.shape[-1])

    stage_in = jnp.concatenate([features, cotangent], axis=1)
    pieces = gather_rounds(stage_in, rows, copies)
    both = reduce_rep(
        local_product(pieces, block_index, block_count, block_values, row_index, copy_index)
    )
    agg_one = both[:, :feature_width].astype(jnp.bfloat16)
    spread_cotangent = both[:, feature_width:]
    carried = lax.dot_general(
        spread_cotangent,
        weight_two.astype(jnp.float32),
        (((1,), (1,)), ((), ())),
        precision=lax.Precision.HIGHEST,
        preferred_element_type=jnp.float32,
    )
    pre_one = jnp.dot(agg_one, weight_one, preferred_element_type=jnp.float32)
    hidden = jax.nn.silu(pre_one).astype(jnp.bfloat16)
    gate_value = jax.nn.sigmoid(pre_one)
    pre_grad = (carried * (gate_value + pre_one * gate_value * (1.0 - gate_value))).astype(
        jnp.bfloat16
    )
    grad_one = lax.dot_general(
        agg_one, pre_grad, (((0,), (0,)), ((), ())), preferred_element_type=jnp.float32
    )
    grad_two = lax.dot_general(
        hidden.astype(jnp.float32),
        spread_cotangent,
        (((0,), (0,)), ((), ())),
        precision=lax.Precision.HIGHEST,
        preferred_element_type=jnp.float32,
    )
    grads = jnp.stack([grad_one, grad_two])
    total = grads.size
    levels = len(all_bits)
    segment = grads.reshape([2] * levels + [total // devices])
    summed = reduce_scatter_bits(segment, me, all_bits, devices)
    grads = all_gather_bits(summed, me, all_bits, devices).reshape(grads.shape)

    hidden_full = gather_rep(hidden)
    pieces_two = gather_rounds(hidden_full, rows, copies)
    agg_two = reduce_rep(
        local_product(pieces_two, block_index, block_count, block_values, row_index, copy_index)
    ).astype(jnp.bfloat16)
    logits = jnp.dot(agg_two, weight_two, preferred_element_type=jnp.float32).astype(jnp.bfloat16)
    return (logits, grads[0], grads[1])


def solution(mesh):
    rows = mesh.shape["row"]
    copies = mesh.shape["rep"]
    if not (is_pow2(rows) and is_pow2(copies) and rows % copies == 0):
        raise ValueError("unsupported mesh")
    in_specs = (
        P("row", None),
        P("row", None),
        P(),
        P(),
        P("row", "rep", None, None),
        P("row", "rep", None),
        P("row", "rep", None, None, None, None),
    )
    out_specs = (P(("row", "rep"), None), P(), P())
    return jax.shard_map(shards, mesh=mesh, in_specs=in_specs, out_specs=out_specs, check_vma=False)
```

```python
import jax
import jax.numpy as jnp
from jax import lax
from jax.sharding import PartitionSpec as P

AXES = ("row", "rep")


def is_pow2(n):
    return n > 0 and (n & (n - 1)) == 0


def bit_pairs(devices, bit):
    return [(d, d ^ (1 << bit)) for d in range(devices)]


def reduce_scatter_bits(y, me, bits, devices):
    for step, bit in enumerate(bits):
        axis = len(bits) - 1 - step
        mine = (me >> bit) & 1
        keep = lax.dynamic_index_in_dim(y, mine, axis, keepdims=False)
        send = lax.dynamic_index_in_dim(y, 1 - mine, axis, keepdims=False)
        y = keep + lax.ppermute(send, AXES, bit_pairs(devices, bit))
    return y


def all_gather_bits(z, me, bits, devices):
    for step, bit in enumerate(reversed(bits)):
        mine = (me >> bit) & 1
        other = lax.ppermute(z, AXES, bit_pairs(devices, bit))
        low = jnp.where(mine == 0, z, other)
        high = jnp.where(mine == 0, other, z)
        z = jnp.stack([low, high], axis=step)
    return z


def group_pairs(devices, mask):
    return [(d, d ^ mask) for d in range(devices)]


def reduce_scatter_groups(y, me, groups, devices):
    levels = sum(len(group) for group in groups)
    rest = y.shape[levels:]
    for group in groups:
        width = len(group)
        size = 1 << width
        low = group[0]
        y = y.reshape(y.shape[: levels - width] + (size,) + rest)
        axis = levels - width
        mine = (me >> low) & (size - 1)
        total = lax.dynamic_index_in_dim(y, mine, axis, keepdims=False)
        for offset in range(1, size):
            send = lax.dynamic_index_in_dim(y, mine ^ offset, axis, keepdims=False)
            total = total + lax.ppermute(send, AXES, group_pairs(devices, offset << low))
        y = total
        levels -= width
    return y


def all_gather_groups(z, me, groups, devices):
    done = 0
    for group in reversed(groups):
        width = len(group)
        size = 1 << width
        low = group[0]
        mine = (me >> low) & (size - 1)
        received = [z]
        for offset in range(1, size):
            received.append(lax.ppermute(z, AXES, group_pairs(devices, offset << low)))
        stacked = jnp.stack(received, axis=done)
        order = jnp.arange(size, dtype=jnp.int32) ^ mine
        z = jnp.take(stacked, order, axis=done)
        z = z.reshape(z.shape[:done] + (2,) * width + z.shape[done + 1 :])
        done += width
    return z


def bit_groups(bits, widest):
    return [bits[i : i + widest] for i in range(0, len(bits), widest)]


def gather_rounds(x, rows, copies):
    sections = rows // copies
    pieces = []
    for t in range(sections):
        pairs = []
        for r in range(rows):
            for c in range(copies):
                q = c * sections + (r + t) % sections
                pairs.append((q * copies + r // sections, r * copies + c))
        pieces.append(lax.ppermute(x, AXES, pairs))
    return jnp.stack(pieces)


def local_product(pieces, block_index, block_count, block_values, row_index, copy_index):
    sections = pieces.shape[0]
    block_rows = block_values.shape[2]
    slot_count = block_values.shape[3]
    block_side = block_values.shape[-1]
    width = pieces.shape[-1]
    panels = pieces.reshape(sections * block_rows, block_side, width)
    local = block_index[0, 0] - copy_index * slot_count
    shard = local // block_rows
    arrival = (shard - row_index) % sections
    columns = arrival * block_rows + local % block_rows
    live_slots = jnp.arange(slot_count, dtype=jnp.int32)[None, :] < block_count[0, 0][:, None]
    picked = jnp.take(panels, columns.reshape(-1), axis=0).reshape(
        block_rows, slot_count, block_side, width
    )
    picked = jnp.where(live_slots[:, :, None, None], picked, jnp.zeros((), picked.dtype))
    partial_value = lax.dot_general(
        block_values[0, 0],
        picked,
        (((1, 3), (1, 2)), ((0,), (0,))),
        preferred_element_type=jnp.float32,
    )
    return partial_value.reshape(block_rows * block_side, width)


def shards(features, cotangent, weight_one, weight_two, block_index, block_count, block_values):
    rows = lax.axis_size("row")
    copies = lax.axis_size("rep")
    row_index = lax.axis_index("row")
    copy_index = lax.axis_index("rep")
    devices = rows * copies
    me = row_index * copies + copy_index
    node_rows, feature_width = features.shape
    share_rows = node_rows // copies
    rep_levels = copies.bit_length() - 1
    rep_bits = list(range(rep_levels))
    all_bits = list(range(devices.bit_length() - 1))

    def reduce_rep(partial_value):
        y = partial_value.reshape([2] * rep_levels + [share_rows, partial_value.shape[-1]])
        return reduce_scatter_bits(y, me, rep_bits, devices)

    def gather_rep(z):
        return all_gather_bits(z, me, rep_bits, devices).reshape(node_rows, z.shape[-1])

    stage_in = jnp.concatenate([features, cotangent], axis=1)
    pieces = gather_rounds(stage_in, rows, copies)
    both = reduce_rep(
        local_product(pieces, block_index, block_count, block_values, row_index, copy_index)
    )
    agg_one = both[:, :feature_width].astype(jnp.bfloat16)
    spread_cotangent = both[:, feature_width:]
    carried = lax.dot_general(
        spread_cotangent,
        weight_two.astype(jnp.float32),
        (((1,), (1,)), ((), ())),
        precision=lax.Precision.HIGHEST,
        preferred_element_type=jnp.float32,
    )
    pre_one = jnp.dot(agg_one, weight_one, preferred_element_type=jnp.float32)
    hidden = jax.nn.silu(pre_one).astype(jnp.bfloat16)
    gate_value = jax.nn.sigmoid(pre_one)
    pre_grad = (carried * (gate_value + pre_one * gate_value * (1.0 - gate_value))).astype(
        jnp.bfloat16
    )
    grad_one = lax.dot_general(
        agg_one, pre_grad, (((0,), (0,)), ((), ())), preferred_element_type=jnp.float32
    )
    grad_two = lax.dot_general(
        hidden.astype(jnp.float32),
        spread_cotangent,
        (((0,), (0,)), ((), ())),
        precision=lax.Precision.HIGHEST,
        preferred_element_type=jnp.float32,
    )
    grads = jnp.stack([grad_one, grad_two])
    total = grads.size
    levels = len(all_bits)
    segment = grads.reshape([2] * levels + [total // devices])
    groups = [[bit] for bit in rep_bits] + bit_groups(all_bits[rep_levels:], 3)
    summed = reduce_scatter_groups(segment, me, groups, devices)
    grads = all_gather_groups(summed, me, groups, devices).reshape(grads.shape)

    hidden_full = gather_rep(hidden)
    pieces_two = gather_rounds(hidden_full, rows, copies)
    agg_two = reduce_rep(
        local_product(pieces_two, block_index, block_count, block_values, row_index, copy_index)
    ).astype(jnp.bfloat16)
    logits = jnp.dot(agg_two, weight_two, preferred_element_type=jnp.float32).astype(jnp.bfloat16)
    return (logits, grads[0], grads[1])


def solution(mesh):
    rows = mesh.shape["row"]
    copies = mesh.shape["rep"]
    if not (is_pow2(rows) and is_pow2(copies) and rows % copies == 0):
        raise ValueError("unsupported mesh")
    in_specs = (
        P("row", None),
        P("row", None),
        P(),
        P(),
        P("row", "rep", None, None),
        P("row", "rep", None),
        P("row", "rep", None, None, None, None),
    )
    out_specs = (P(("row", "rep"), None), P(), P())
    return jax.shard_map(shards, mesh=mesh, in_specs=in_specs, out_specs=out_specs, check_vma=False)
```

```python
import jax
import jax.numpy as jnp
from jax import lax
from jax.sharding import PartitionSpec as P

AXES = ("row", "rep")


def is_pow2(n):
    return n > 0 and (n & (n - 1)) == 0


def bit_pairs(devices, bit):
    return [(d, d ^ (1 << bit)) for d in range(devices)]


def group_pairs(devices, mask):
    return [(d, d ^ mask) for d in range(devices)]


def reduce_scatter_bits(y, me, bits, devices):
    for step, bit in enumerate(bits):
        axis = len(bits) - 1 - step
        mine = (me >> bit) & 1
        keep = lax.dynamic_index_in_dim(y, mine, axis, keepdims=False)
        send = lax.dynamic_index_in_dim(y, 1 - mine, axis, keepdims=False)
        y = keep + lax.ppermute(send, AXES, bit_pairs(devices, bit))
    return y


def all_gather_bits(z, me, bits, devices):
    for step, bit in enumerate(reversed(bits)):
        mine = (me >> bit) & 1
        other = lax.ppermute(z, AXES, bit_pairs(devices, bit))
        low = jnp.where(mine == 0, z, other)
        high = jnp.where(mine == 0, other, z)
        z = jnp.stack([low, high], axis=step)
    return z


def gather_rounds(x, rows, copies):
    sections = rows // copies
    pieces = []
    for t in range(sections):
        pairs = []
        for r in range(rows):
            for c in range(copies):
                q = c * sections + (r + t) % sections
                pairs.append((q * copies + r // sections, r * copies + c))
        pieces.append(lax.ppermute(x, AXES, pairs))
    return jnp.stack(pieces)


def local_product(pieces, block_index, block_count, block_values, row_index, copy_index):
    sections = pieces.shape[0]
    block_rows = block_values.shape[2]
    slot_count = block_values.shape[3]
    block_side = block_values.shape[-1]
    width = pieces.shape[-1]
    panels = pieces.reshape(sections * block_rows, block_side, width)
    local = block_index[0, 0] - copy_index * slot_count
    shard = local // block_rows
    arrival = (shard - row_index) % sections
    columns = arrival * block_rows + local % block_rows
    live_slots = jnp.arange(slot_count, dtype=jnp.int32)[None, :] < block_count[0, 0][:, None]
    picked = jnp.take(panels, columns.reshape(-1), axis=0).reshape(
        block_rows, slot_count, block_side, width
    )
    picked = jnp.where(live_slots[:, :, None, None], picked, jnp.zeros((), picked.dtype))
    partial_value = lax.dot_general(
        block_values[0, 0],
        picked,
        (((1, 3), (1, 2)), ((0,), (0,))),
        preferred_element_type=jnp.float32,
    )
    return partial_value.reshape(block_rows * block_side, width)


def halve(y, mine):
    half = y.shape[0] // 2
    keep = lax.dynamic_slice_in_dim(y, mine * half, half, 0)
    send = lax.dynamic_slice_in_dim(y, (1 - mine) * half, half, 0)
    return keep, send


def join(z, other, mine, axis, stack):
    low = jnp.where(mine == 0, z, other)
    high = jnp.where(mine == 0, other, z)
    if stack:
        return jnp.stack([low, high], axis=axis)
    return jnp.concatenate([low, high], axis=axis)


def exchange(pieces, mask, devices, width):
    flat = [p.reshape(-1, width) for p in pieces]
    sizes = [f.shape[0] for f in flat]
    got = lax.ppermute(jnp.concatenate(flat, axis=0), AXES, group_pairs(devices, mask))
    out, at = [], 0
    for p, n in zip(pieces, sizes):
        out.append(got[at : at + n].reshape(p.shape))
        at += n
    return out


def shards(features, cotangent, weight_one, weight_two, block_index, block_count, block_values):
    rows = lax.axis_size("row")
    copies = lax.axis_size("rep")
    row_index = lax.axis_index("row")
    copy_index = lax.axis_index("rep")
    devices = rows * copies
    me = row_index * copies + copy_index
    node_rows, feature_width = features.shape
    share_rows = node_rows // copies
    rep_levels = copies.bit_length() - 1
    rep_bits = list(range(rep_levels))
    levels = devices.bit_length() - 1
    grad_elems = feature_width * feature_width
    width = feature_width if grad_elems // feature_width >= 8 * devices else grad_elems // (8 * devices)
    my_bit = [(me >> b) & 1 for b in range(levels)]

    stage_in = jnp.concatenate([features, cotangent], axis=1)
    pieces = gather_rounds(stage_in, rows, copies)
    partial_a = local_product(pieces, block_index, block_count, block_values, row_index, copy_index)
    partial_a = partial_a.reshape([2] * rep_levels + [share_rows, partial_a.shape[-1]])
    both = reduce_scatter_bits(partial_a, me, rep_bits, devices)
    agg_one = both[:, :feature_width].astype(jnp.bfloat16)
    spread_cotangent = both[:, feature_width:]
    carried = lax.dot_general(
        spread_cotangent,
        weight_two.astype(jnp.float32),
        (((1,), (1,)), ((), ())),
        precision=lax.Precision.HIGHEST,
        preferred_element_type=jnp.float32,
    )
    pre_one = jnp.dot(agg_one, weight_one, preferred_element_type=jnp.float32)
    hidden = jax.nn.silu(pre_one).astype(jnp.bfloat16)
    gate_value = jax.nn.sigmoid(pre_one)
    pre_grad = (carried * (gate_value + pre_one * gate_value * (1.0 - gate_value))).astype(
        jnp.bfloat16
    )
    grad_one = lax.dot_general(
        agg_one, pre_grad, (((0,), (0,)), ((), ())), preferred_element_type=jnp.float32
    )
    grad_two = lax.dot_general(
        hidden.astype(jnp.float32),
        spread_cotangent,
        (((0,), (0,)), ((), ())),
        precision=lax.Precision.HIGHEST,
        preferred_element_type=jnp.float32,
    )
    grads = [g.reshape(-1, width) for g in (grad_one, grad_two)]

    grad_order = list(reversed(rep_bits)) + list(range(rep_levels, levels))
    held = hidden.astype(jnp.float32)
    for step, bit in enumerate(reversed(rep_bits)):
        halves = [halve(g, my_bit[bit]) for g in grads]
        got = exchange([held] + [h[1] for h in halves], 1 << bit, devices, width)
        held = join(held, got[0], my_bit[bit], step, True)
        grads = [h[0] + r for h, r in zip(halves, got[1:])]
    hidden_full = held.reshape(node_rows, feature_width).astype(jnp.bfloat16)
    for bit in grad_order[rep_levels:]:
        halves = [halve(g, my_bit[bit]) for g in grads]
        got = exchange([h[1] for h in halves], 1 << bit, devices, width)
        grads = [h[0] + r for h, r in zip(halves, got)]
    for bit in reversed(grad_order[rep_levels:]):
        got = exchange(grads, 1 << bit, devices, width)
        grads = [join(g, r, my_bit[bit], 0, False) for g, r in zip(grads, got)]

    pieces_two = gather_rounds(hidden_full, rows, copies)
    partial_b = local_product(pieces_two, block_index, block_count, block_values, row_index, copy_index)
    partial_b = partial_b.reshape([2] * rep_levels + [share_rows, feature_width])
    for step, bit in enumerate(rep_bits):
        axis = rep_levels - 1 - step
        keep = lax.dynamic_index_in_dim(partial_b, my_bit[bit], axis, keepdims=False)
        send = lax.dynamic_index_in_dim(partial_b, 1 - my_bit[bit], axis, keepdims=False)
        got = exchange([send] + grads, 1 << bit, devices, width)
        partial_b = keep + got[0]
        grads = [join(g, r, my_bit[bit], 0, False) for g, r in zip(grads, got[1:])]
    agg_two = partial_b.astype(jnp.bfloat16)
    logits = jnp.dot(agg_two, weight_two, preferred_element_type=jnp.float32).astype(jnp.bfloat16)
    grad_one, grad_two = [g.reshape(feature_width, feature_width) for g in grads]
    return (logits, grad_one, grad_two)


def solution(mesh):
    rows = mesh.shape["row"]
    copies = mesh.shape["rep"]
    if not (is_pow2(rows) and is_pow2(copies) and rows % copies == 0):
        raise ValueError("unsupported mesh")
    in_specs = (
        P("row", None),
        P("row", None),
        P(),
        P(),
        P("row", "rep", None, None),
        P("row", "rep", None),
        P("row", "rep", None, None, None, None),
    )
    out_specs = (P(("row", "rep"), None), P(), P())
    return jax.shard_map(shards, mesh=mesh, in_specs=in_specs, out_specs=out_specs, check_vma=False)
```

```python
import jax
import jax.numpy as jnp
from jax import lax
from jax.sharding import PartitionSpec as P

AXES = ("row", "rep")


def is_pow2(n):
    return n > 0 and (n & (n - 1)) == 0


def bit_pairs(devices, bit):
    return [(d, d ^ (1 << bit)) for d in range(devices)]


def reduce_scatter_bits(y, me, bits, devices):
    for step, bit in enumerate(bits):
        axis = len(bits) - 1 - step
        mine = (me >> bit) & 1
        keep = lax.dynamic_index_in_dim(y, mine, axis, keepdims=False)
        send = lax.dynamic_index_in_dim(y, 1 - mine, axis, keepdims=False)
        y = keep + lax.ppermute(send, AXES, bit_pairs(devices, bit))
    return y


def all_gather_bits(z, me, bits, devices):
    for step, bit in enumerate(reversed(bits)):
        mine = (me >> bit) & 1
        other = lax.ppermute(z, AXES, bit_pairs(devices, bit))
        low = jnp.where(mine == 0, z, other)
        high = jnp.where(mine == 0, other, z)
        z = jnp.stack([low, high], axis=step)
    return z


def gather_rounds(x, rows, copies):
    sections = rows // copies
    pieces = []
    for t in range(sections):
        pairs = []
        for r in range(rows):
            for c in range(copies):
                q = c * sections + (r + t) % sections
                pairs.append((q * copies + r // sections, r * copies + c))
        pieces.append(lax.ppermute(x, AXES, pairs))
    return jnp.stack(pieces)


def local_product(pieces, block_index, block_count, block_values, row_index, copy_index):
    sections = pieces.shape[0]
    block_rows = block_values.shape[2]
    slot_count = block_values.shape[3]
    block_side = block_values.shape[-1]
    width = pieces.shape[-1]
    panels = pieces.reshape(sections * block_rows, block_side, width)
    local = block_index[0, 0] - copy_index * slot_count
    shard = local // block_rows
    arrival = (shard - row_index) % sections
    columns = arrival * block_rows + local % block_rows
    live_slots = jnp.arange(slot_count, dtype=jnp.int32)[None, :] < block_count[0, 0][:, None]
    picked = jnp.take(panels, columns.reshape(-1), axis=0).reshape(
        block_rows, slot_count, block_side, width
    )
    picked = jnp.where(live_slots[:, :, None, None], picked, jnp.zeros((), picked.dtype))
    partial_value = lax.dot_general(
        block_values[0, 0],
        picked,
        (((1, 3), (1, 2)), ((0,), (0,))),
        preferred_element_type=jnp.float32,
    )
    return partial_value.reshape(block_rows * block_side, width)


def shards(features, cotangent, weight_one, weight_two, block_index, block_count, block_values):
    rows = lax.axis_size("row")
    copies = lax.axis_size("rep")
    row_index = lax.axis_index("row")
    copy_index = lax.axis_index("rep")
    devices = rows * copies
    me = row_index * copies + copy_index
    node_rows, feature_width = features.shape
    share_rows = node_rows // copies
    rep_levels = copies.bit_length() - 1
    rep_bits = list(range(rep_levels))
    all_bits = list(range(devices.bit_length() - 1))

    def reduce_rep(partial_value):
        y = partial_value.reshape([2] * rep_levels + [share_rows, partial_value.shape[-1]])
        return reduce_scatter_bits(y, me, rep_bits, devices)

    def gather_rep(z):
        return all_gather_bits(z, me, rep_bits, devices).reshape(node_rows, z.shape[-1])

    stage_in = jnp.concatenate([features, cotangent], axis=1)
    pieces = gather_rounds(stage_in, rows, copies)
    both = reduce_rep(
        local_product(pieces, block_index, block_count, block_values, row_index, copy_index)
    )
    agg_one = both[:, :feature_width].astype(jnp.bfloat16)
    spread_cotangent = both[:, feature_width:]
    carried = lax.dot_general(
        spread_cotangent,
        weight_two.astype(jnp.float32),
        (((1,), (1,)), ((), ())),
        precision=lax.Precision.HIGHEST,
        preferred_element_type=jnp.float32,
    )
    pre_one = jnp.dot(agg_one, weight_one, preferred_element_type=jnp.float32)
    hidden = jax.nn.silu(pre_one).astype(jnp.bfloat16)
    gate_value = jax.nn.sigmoid(pre_one)
    pre_grad = (carried * (gate_value + pre_one * gate_value * (1.0 - gate_value))).astype(
        jnp.bfloat16
    )
    grad_one = lax.dot_general(
        agg_one, pre_grad, (((0,), (0,)), ((), ())), preferred_element_type=jnp.float32
    )
    grad_two = lax.dot_general(
        hidden.astype(jnp.float32),
        spread_cotangent,
        (((0,), (0,)), ((), ())),
        precision=lax.Precision.HIGHEST,
        preferred_element_type=jnp.float32,
    )
    grads = jnp.concatenate([grad_one, grad_two], axis=0)
    grad_rows = grads.shape[0] // copies
    quarter = reduce_scatter_bits(
        grads.reshape([2] * rep_levels + [grad_rows, feature_width]), me, rep_bits, devices
    )
    if grad_rows % rows == 0:
        parts = quarter.reshape(rows, grad_rows // rows, feature_width)
    else:
        parts = quarter.reshape(rows, -1)
    mine = lax.all_to_all(parts, "row", 0, 0, tiled=False).sum(axis=0)
    spread = lax.all_to_all(jnp.broadcast_to(mine, parts.shape), "row", 0, 0, tiled=False)
    quarter = spread.reshape(grad_rows, feature_width)
    grads = all_gather_bits(quarter, me, rep_bits, devices).reshape(grads.shape)

    hidden_full = gather_rep(hidden)
    pieces_two = gather_rounds(hidden_full, rows, copies)
    agg_two = reduce_rep(
        local_product(pieces_two, block_index, block_count, block_values, row_index, copy_index)
    ).astype(jnp.bfloat16)
    logits = jnp.dot(agg_two, weight_two, preferred_element_type=jnp.float32).astype(jnp.bfloat16)
    return (logits, grads[:feature_width], grads[feature_width:])


def solution(mesh):
    rows = mesh.shape["row"]
    copies = mesh.shape["rep"]
    if not (is_pow2(rows) and is_pow2(copies) and rows % copies == 0):
        raise ValueError("unsupported mesh")
    in_specs = (
        P("row", None),
        P("row", None),
        P(),
        P(),
        P("row", "rep", None, None),
        P("row", "rep", None),
        P("row", "rep", None, None, None, None),
    )
    out_specs = (P(("row", "rep"), None), P(), P())
    return jax.shard_map(shards, mesh=mesh, in_specs=in_specs, out_specs=out_specs, check_vma=False)
```

```python
import jax
import jax.numpy as jnp
from jax import lax
from jax.sharding import PartitionSpec as P

AXES = ("row", "rep")


def is_pow2(n):
    return n > 0 and (n & (n - 1)) == 0


def bit_pairs(devices, bit):
    return [(d, d ^ (1 << bit)) for d in range(devices)]


def reduce_scatter_bits(y, me, bits, devices):
    for step, bit in enumerate(bits):
        axis = len(bits) - 1 - step
        mine = (me >> bit) & 1
        keep = lax.dynamic_index_in_dim(y, mine, axis, keepdims=False)
        send = lax.dynamic_index_in_dim(y, 1 - mine, axis, keepdims=False)
        y = keep + lax.ppermute(send, AXES, bit_pairs(devices, bit))
    return y


def all_gather_bits(z, me, bits, devices):
    for step, bit in enumerate(reversed(bits)):
        mine = (me >> bit) & 1
        other = lax.ppermute(z, AXES, bit_pairs(devices, bit))
        low = jnp.where(mine == 0, z, other)
        high = jnp.where(mine == 0, other, z)
        z = jnp.stack([low, high], axis=step)
    return z


def gather_rounds(x, rows, copies):
    sections = rows // copies
    pieces = []
    for t in range(sections):
        pairs = []
        for r in range(rows):
            for c in range(copies):
                q = c * sections + (r + t) % sections
                source = (r // sections + t + c) % copies
                pairs.append((q * copies + source, r * copies + c))
        pieces.append(lax.ppermute(x, AXES, pairs))
    return jnp.stack(pieces)


def local_product(pieces, block_index, block_count, block_values, row_index, copy_index):
    sections = pieces.shape[0]
    block_rows = block_values.shape[2]
    slot_count = block_values.shape[3]
    block_side = block_values.shape[-1]
    width = pieces.shape[-1]
    panels = pieces.reshape(sections * block_rows, block_side, width)
    local = block_index[0, 0] - copy_index * slot_count
    shard = local // block_rows
    arrival = (shard - row_index) % sections
    columns = arrival * block_rows + local % block_rows
    live_slots = jnp.arange(slot_count, dtype=jnp.int32)[None, :] < block_count[0, 0][:, None]
    picked = jnp.take(panels, columns.reshape(-1), axis=0).reshape(
        block_rows, slot_count, block_side, width
    )
    picked = jnp.where(live_slots[:, :, None, None], picked, jnp.zeros((), picked.dtype))
    partial_value = lax.dot_general(
        block_values[0, 0],
        picked,
        (((1, 3), (1, 2)), ((0,), (0,))),
        preferred_element_type=jnp.float32,
    )
    return partial_value.reshape(block_rows * block_side, width)


def shards(features, cotangent, weight_one, weight_two, block_index, block_count, block_values):
    rows = lax.axis_size("row")
    copies = lax.axis_size("rep")
    row_index = lax.axis_index("row")
    copy_index = lax.axis_index("rep")
    devices = rows * copies
    me = row_index * copies + copy_index
    node_rows, feature_width = features.shape
    share_rows = node_rows // copies
    rep_levels = copies.bit_length() - 1
    rep_bits = list(range(rep_levels))
    all_bits = list(range(devices.bit_length() - 1))

    def reduce_rep(partial_value):
        y = partial_value.reshape([2] * rep_levels + [share_rows, partial_value.shape[-1]])
        return reduce_scatter_bits(y, me, rep_bits, devices)

    def gather_rep(z):
        return all_gather_bits(z, me, rep_bits, devices).reshape(node_rows, z.shape[-1])

    stage_in = jnp.concatenate([features, cotangent], axis=1)
    pieces = gather_rounds(stage_in, rows, copies)
    both = reduce_rep(
        local_product(pieces, block_index, block_count, block_values, row_index, copy_index)
    )
    agg_one = both[:, :feature_width].astype(jnp.bfloat16)
    spread_cotangent = both[:, feature_width:]
    carried = lax.dot_general(
        spread_cotangent,
        weight_two.astype(jnp.float32),
        (((1,), (1,)), ((), ())),
        precision=lax.Precision.HIGHEST,
        preferred_element_type=jnp.float32,
    )
    pre_one = jnp.dot(agg_one, weight_one, preferred_element_type=jnp.float32)
    hidden = jax.nn.silu(pre_one).astype(jnp.bfloat16)
    gate_value = jax.nn.sigmoid(pre_one)
    pre_grad = (carried * (gate_value + pre_one * gate_value * (1.0 - gate_value))).astype(
        jnp.bfloat16
    )
    grad_one = lax.dot_general(
        agg_one, pre_grad, (((0,), (0,)), ((), ())), preferred_element_type=jnp.float32
    )
    grad_two = lax.dot_general(
        hidden.astype(jnp.float32),
        spread_cotangent,
        (((0,), (0,)), ((), ())),
        precision=lax.Precision.HIGHEST,
        preferred_element_type=jnp.float32,
    )
    grads = jnp.concatenate([grad_one, grad_two], axis=0)
    grad_rows = grads.shape[0] // copies
    quarter = reduce_scatter_bits(
        grads.reshape([2] * rep_levels + [grad_rows, feature_width]), me, rep_bits, devices
    )
    if grad_rows % rows == 0:
        parts = quarter.reshape(rows, grad_rows // rows, feature_width)
    else:
        parts = quarter.reshape(rows, -1)
    mine = lax.all_to_all(parts, "row", 0, 0, tiled=False).sum(axis=0)
    spread = lax.all_to_all(jnp.broadcast_to(mine, parts.shape), "row", 0, 0, tiled=False)
    quarter = spread.reshape(grad_rows, feature_width)
    grads = all_gather_bits(quarter, me, rep_bits, devices).reshape(grads.shape)

    hidden_full = gather_rep(hidden)
    pieces_two = gather_rounds(hidden_full, rows, copies)
    agg_two = reduce_rep(
        local_product(pieces_two, block_index, block_count, block_values, row_index, copy_index)
    ).astype(jnp.bfloat16)
    logits = jnp.dot(agg_two, weight_two, preferred_element_type=jnp.float32).astype(jnp.bfloat16)
    return (logits, grads[:feature_width], grads[feature_width:])


def solution(mesh):
    rows = mesh.shape["row"]
    copies = mesh.shape["rep"]
    if not (is_pow2(rows) and is_pow2(copies) and rows % copies == 0):
        raise ValueError("unsupported mesh")
    in_specs = (
        P("row", None),
        P("row", None),
        P(),
        P(),
        P("row", "rep", None, None),
        P("row", "rep", None),
        P("row", "rep", None, None, None, None),
    )
    out_specs = (P(("row", "rep"), None), P(), P())
    return jax.shard_map(shards, mesh=mesh, in_specs=in_specs, out_specs=out_specs, check_vma=False)
```

```python
import jax
import jax.numpy as jnp
from jax import lax
from jax.sharding import PartitionSpec as P

AXES = ("row", "rep")


def is_pow2(n):
    return n > 0 and (n & (n - 1)) == 0


def bit_pairs(devices, bit):
    return [(d, d ^ (1 << bit)) for d in range(devices)]


def reduce_scatter_bits(y, me, bits, devices):
    for step, bit in enumerate(bits):
        axis = len(bits) - 1 - step
        mine = (me >> bit) & 1
        keep = lax.dynamic_index_in_dim(y, mine, axis, keepdims=False)
        send = lax.dynamic_index_in_dim(y, 1 - mine, axis, keepdims=False)
        y = keep + lax.ppermute(send, AXES, bit_pairs(devices, bit))
    return y


def all_gather_bits(z, me, bits, devices):
    for step, bit in enumerate(reversed(bits)):
        mine = (me >> bit) & 1
        other = lax.ppermute(z, AXES, bit_pairs(devices, bit))
        low = jnp.where(mine == 0, z, other)
        high = jnp.where(mine == 0, other, z)
        z = jnp.stack([low, high], axis=step)
    return z


def gather_rounds(x, rows, copies):
    sections = rows // copies
    pieces = []
    for t in range(sections):
        pairs = []
        for r in range(rows):
            for c in range(copies):
                q = c * sections + (r + t) % sections
                source = (r // sections + t + c) % copies
                pairs.append((q * copies + source, r * copies + c))
        pieces.append(lax.ppermute(x, AXES, pairs))
    return jnp.stack(pieces)


def local_product(pieces, block_index, block_count, block_values, row_index, copy_index):
    sections = pieces.shape[0]
    block_rows = block_values.shape[2]
    slot_count = block_values.shape[3]
    block_side = block_values.shape[-1]
    width = pieces.shape[-1]
    panels = pieces.reshape(sections * block_rows, block_side, width)
    local = block_index[0, 0] - copy_index * slot_count
    shard = local // block_rows
    arrival = (shard - row_index) % sections
    columns = arrival * block_rows + local % block_rows
    live_slots = jnp.arange(slot_count, dtype=jnp.int32)[None, :] < block_count[0, 0][:, None]
    picked = jnp.take(panels, columns.reshape(-1), axis=0).reshape(
        block_rows, slot_count, block_side, width
    )
    picked = jnp.where(live_slots[:, :, None, None], picked, jnp.zeros((), picked.dtype))
    partial_value = lax.dot_general(
        block_values[0, 0],
        picked,
        (((1, 3), (1, 2)), ((0,), (0,))),
        preferred_element_type=jnp.float32,
    )
    return partial_value.reshape(block_rows * block_side, width)


def shards(features, cotangent, weight_one, weight_two, block_index, block_count, block_values):
    rows = lax.axis_size("row")
    copies = lax.axis_size("rep")
    row_index = lax.axis_index("row")
    copy_index = lax.axis_index("rep")
    devices = rows * copies
    me = row_index * copies + copy_index
    node_rows, feature_width = features.shape
    share_rows = node_rows // copies
    rep_levels = copies.bit_length() - 1
    rep_bits = list(range(rep_levels))
    all_bits = list(range(devices.bit_length() - 1))

    def reduce_rep(partial_value):
        y = partial_value.reshape([2] * rep_levels + [share_rows, partial_value.shape[-1]])
        return reduce_scatter_bits(y, me, rep_bits, devices)

    def gather_rep(z):
        return all_gather_bits(z, me, rep_bits, devices).reshape(node_rows, z.shape[-1])

    stage_in = jnp.concatenate([features, cotangent], axis=1)
    pieces = gather_rounds(stage_in, rows, copies)
    both = reduce_rep(
        local_product(pieces, block_index, block_count, block_values, row_index, copy_index)
    )
    agg_one = both[:, :feature_width].astype(jnp.bfloat16)
    spread_cotangent = both[:, feature_width:]
    carried = lax.dot_general(
        spread_cotangent,
        weight_two.astype(jnp.float32),
        (((1,), (1,)), ((), ())),
        precision=lax.Precision.HIGHEST,
        preferred_element_type=jnp.float32,
    )
    pre_one = jnp.dot(agg_one, weight_one, preferred_element_type=jnp.float32)
    hidden = jax.nn.silu(pre_one).astype(jnp.bfloat16)
    gate_value = jax.nn.sigmoid(pre_one)
    pre_grad = (carried * (gate_value + pre_one * gate_value * (1.0 - gate_value))).astype(
        jnp.bfloat16
    )
    grad_one = lax.dot_general(
        agg_one, pre_grad, (((0,), (0,)), ((), ())), preferred_element_type=jnp.float32
    )
    grad_two = lax.dot_general(
        hidden.astype(jnp.float32),
        spread_cotangent,
        (((0,), (0,)), ((), ())),
        precision=lax.Precision.HIGHEST,
        preferred_element_type=jnp.float32,
    )
    hidden_full = gather_rep(hidden)
    grads = jnp.concatenate([grad_one, grad_two], axis=0)
    grad_rows = grads.shape[0] // copies
    quarter = reduce_scatter_bits(
        grads.reshape([2] * rep_levels + [grad_rows, feature_width]), me, rep_bits, devices
    )
    hidden_full, quarter = lax.optimization_barrier((hidden_full, quarter))
    pieces_two = gather_rounds(hidden_full, rows, copies)
    if grad_rows % rows == 0:
        parts = quarter.reshape(rows, grad_rows // rows, feature_width)
    else:
        parts = quarter.reshape(rows, -1)
    mine = lax.all_to_all(parts, "row", 0, 0, tiled=False).sum(axis=0)
    spread = lax.all_to_all(jnp.broadcast_to(mine, parts.shape), "row", 0, 0, tiled=False)
    quarter = spread.reshape(grad_rows, feature_width)
    grads = all_gather_bits(quarter, me, rep_bits, devices).reshape(grads.shape)

    agg_two = reduce_rep(
        local_product(pieces_two, block_index, block_count, block_values, row_index, copy_index)
    ).astype(jnp.bfloat16)
    logits = jnp.dot(agg_two, weight_two, preferred_element_type=jnp.float32).astype(jnp.bfloat16)
    return (logits, grads[:feature_width], grads[feature_width:])


def solution(mesh):
    rows = mesh.shape["row"]
    copies = mesh.shape["rep"]
    if not (is_pow2(rows) and is_pow2(copies) and rows % copies == 0):
        raise ValueError("unsupported mesh")
    in_specs = (
        P("row", None),
        P("row", None),
        P(),
        P(),
        P("row", "rep", None, None),
        P("row", "rep", None),
        P("row", "rep", None, None, None, None),
    )
    out_specs = (P(("row", "rep"), None), P(), P())
    return jax.shard_map(shards, mesh=mesh, in_specs=in_specs, out_specs=out_specs, check_vma=False)
```

```python
import jax
import jax.numpy as jnp
from jax import lax
from jax.sharding import PartitionSpec as P

AXES = ("row", "rep")


def is_pow2(n):
    return n > 0 and (n & (n - 1)) == 0


def bit_pairs(devices, bit):
    return [(d, d ^ (1 << bit)) for d in range(devices)]


def group_pairs(devices, mask):
    return [(d, d ^ mask) for d in range(devices)]


def halve(y, mine):
    half = y.shape[0] // 2
    keep = lax.dynamic_slice_in_dim(y, mine * half, half, 0)
    send = lax.dynamic_slice_in_dim(y, (1 - mine) * half, half, 0)
    return keep, send


def join(z, other, mine, axis, stack):
    low = jnp.where(mine == 0, z, other)
    high = jnp.where(mine == 0, other, z)
    if stack:
        return jnp.stack([low, high], axis=axis)
    return jnp.concatenate([low, high], axis=axis)


def exchange(pieces, mask, devices, width):
    flat = [p.reshape(-1, width) for p in pieces]
    sizes = [f.shape[0] for f in flat]
    got = lax.ppermute(jnp.concatenate(flat, axis=0), AXES, group_pairs(devices, mask))
    out, at = [], 0
    for p, n in zip(pieces, sizes):
        out.append(got[at : at + n].reshape(p.shape))
        at += n
    return out


def reduce_scatter_bits(y, me, bits, devices):
    for step, bit in enumerate(bits):
        axis = len(bits) - 1 - step
        mine = (me >> bit) & 1
        keep = lax.dynamic_index_in_dim(y, mine, axis, keepdims=False)
        send = lax.dynamic_index_in_dim(y, 1 - mine, axis, keepdims=False)
        y = keep + lax.ppermute(send, AXES, bit_pairs(devices, bit))
    return y


def all_gather_bits(z, me, bits, devices):
    for step, bit in enumerate(reversed(bits)):
        mine = (me >> bit) & 1
        other = lax.ppermute(z, AXES, bit_pairs(devices, bit))
        low = jnp.where(mine == 0, z, other)
        high = jnp.where(mine == 0, other, z)
        z = jnp.stack([low, high], axis=step)
    return z


def gather_rounds(x, rows, copies):
    sections = rows // copies
    pieces = []
    for t in range(sections):
        pairs = []
        for r in range(rows):
            for c in range(copies):
                q = c * sections + (r + t) % sections
                source = (r // sections + t + c) % copies
                pairs.append((q * copies + source, r * copies + c))
        pieces.append(lax.ppermute(x, AXES, pairs))
    return jnp.stack(pieces)


def local_product(pieces, block_index, block_count, block_values, row_index, copy_index):
    sections = pieces.shape[0]
    block_rows = block_values.shape[2]
    slot_count = block_values.shape[3]
    block_side = block_values.shape[-1]
    width = pieces.shape[-1]
    panels = pieces.reshape(sections * block_rows, block_side, width)
    local = block_index[0, 0] - copy_index * slot_count
    shard = local // block_rows
    arrival = (shard - row_index) % sections
    columns = arrival * block_rows + local % block_rows
    live_slots = jnp.arange(slot_count, dtype=jnp.int32)[None, :] < block_count[0, 0][:, None]
    picked = jnp.take(panels, columns.reshape(-1), axis=0).reshape(
        block_rows, slot_count, block_side, width
    )
    picked = jnp.where(live_slots[:, :, None, None], picked, jnp.zeros((), picked.dtype))
    partial_value = lax.dot_general(
        block_values[0, 0],
        picked,
        (((1, 3), (1, 2)), ((0,), (0,))),
        preferred_element_type=jnp.float32,
    )
    return partial_value.reshape(block_rows * block_side, width)


def shards(features, cotangent, weight_one, weight_two, block_index, block_count, block_values):
    rows = lax.axis_size("row")
    copies = lax.axis_size("rep")
    row_index = lax.axis_index("row")
    copy_index = lax.axis_index("rep")
    devices = rows * copies
    me = row_index * copies + copy_index
    node_rows, feature_width = features.shape
    share_rows = node_rows // copies
    rep_levels = copies.bit_length() - 1
    rep_bits = list(range(rep_levels))
    all_bits = list(range(devices.bit_length() - 1))

    def reduce_rep(partial_value):
        y = partial_value.reshape([2] * rep_levels + [share_rows, partial_value.shape[-1]])
        return reduce_scatter_bits(y, me, rep_bits, devices)

    def gather_rep(z):
        return all_gather_bits(z, me, rep_bits, devices).reshape(node_rows, z.shape[-1])

    stage_in = jnp.concatenate([features, cotangent], axis=1)
    pieces = gather_rounds(stage_in, rows, copies)
    both = reduce_rep(
        local_product(pieces, block_index, block_count, block_values, row_index, copy_index)
    )
    agg_one = both[:, :feature_width].astype(jnp.bfloat16)
    spread_cotangent = both[:, feature_width:]
    carried = lax.dot_general(
        spread_cotangent,
        weight_two.astype(jnp.float32),
        (((1,), (1,)), ((), ())),
        precision=lax.Precision.HIGHEST,
        preferred_element_type=jnp.float32,
    )
    pre_one = jnp.dot(agg_one, weight_one, preferred_element_type=jnp.float32)
    hidden = jax.nn.silu(pre_one).astype(jnp.bfloat16)
    gate_value = jax.nn.sigmoid(pre_one)
    pre_grad = (carried * (gate_value + pre_one * gate_value * (1.0 - gate_value))).astype(
        jnp.bfloat16
    )
    grad_one = lax.dot_general(
        agg_one, pre_grad, (((0,), (0,)), ((), ())), preferred_element_type=jnp.float32
    )
    grad_two = lax.dot_general(
        hidden.astype(jnp.float32),
        spread_cotangent,
        (((0,), (0,)), ((), ())),
        precision=lax.Precision.HIGHEST,
        preferred_element_type=jnp.float32,
    )
    my_bit = [(me >> b) & 1 for b in range(rep_levels)]
    grads = jnp.concatenate([grad_one, grad_two], axis=0)
    held = hidden.astype(jnp.float32)
    for step, bit in enumerate(reversed(rep_bits)):
        keep, send = halve(grads, my_bit[bit])
        got = exchange([held, send], 1 << bit, devices, feature_width)
        held = join(held, got[0], my_bit[bit], step, True)
        grads = keep + got[1]
    hidden_full = held.reshape(node_rows, feature_width).astype(jnp.bfloat16)
    pieces_two = gather_rounds(hidden_full, rows, copies)
    grad_rows = grads.shape[0]
    if grad_rows % rows == 0:
        parts = grads.reshape(rows, grad_rows // rows, feature_width)
    else:
        parts = grads.reshape(rows, -1)
    mine = lax.all_to_all(parts, "row", 0, 0, tiled=False).sum(axis=0)
    spread = lax.all_to_all(jnp.broadcast_to(mine, parts.shape), "row", 0, 0, tiled=False)
    grads = spread.reshape(grad_rows, feature_width)
    partial_b = local_product(pieces_two, block_index, block_count, block_values, row_index, copy_index)
    partial_b = partial_b.reshape([2] * rep_levels + [share_rows, feature_width])
    for step, bit in enumerate(rep_bits):
        axis = rep_levels - 1 - step
        keep = lax.dynamic_index_in_dim(partial_b, my_bit[bit], axis, keepdims=False)
        send = lax.dynamic_index_in_dim(partial_b, 1 - my_bit[bit], axis, keepdims=False)
        got = exchange([send, grads], 1 << bit, devices, feature_width)
        partial_b = keep + got[0]
        grads = join(grads, got[1], my_bit[bit], 0, False)
    agg_two = partial_b.astype(jnp.bfloat16)
    logits = jnp.dot(agg_two, weight_two, preferred_element_type=jnp.float32).astype(jnp.bfloat16)
    return (logits, grads[:feature_width], grads[feature_width:])


def solution(mesh):
    rows = mesh.shape["row"]
    copies = mesh.shape["rep"]
    if not (is_pow2(rows) and is_pow2(copies) and rows % copies == 0):
        raise ValueError("unsupported mesh")
    in_specs = (
        P("row", None),
        P("row", None),
        P(),
        P(),
        P("row", "rep", None, None),
        P("row", "rep", None),
        P("row", "rep", None, None, None, None),
    )
    out_specs = (P(("row", "rep"), None), P(), P())
    return jax.shard_map(shards, mesh=mesh, in_specs=in_specs, out_specs=out_specs, check_vma=False)
```

```python
import jax
import jax.numpy as jnp
from jax import lax
from jax.sharding import PartitionSpec as P

AXES = ("row", "rep")


def is_pow2(n):
    return n > 0 and (n & (n - 1)) == 0


def bit_pairs(devices, bit):
    return [(d, d ^ (1 << bit)) for d in range(devices)]


def reduce_scatter_bits(y, me, bits, devices):
    for step, bit in enumerate(bits):
        axis = len(bits) - 1 - step
        mine = (me >> bit) & 1
        keep = lax.dynamic_index_in_dim(y, mine, axis, keepdims=False)
        send = lax.dynamic_index_in_dim(y, 1 - mine, axis, keepdims=False)
        y = keep + lax.ppermute(send, AXES, bit_pairs(devices, bit))
    return y


def all_gather_bits(z, me, bits, devices):
    for step, bit in enumerate(reversed(bits)):
        mine = (me >> bit) & 1
        other = lax.ppermute(z, AXES, bit_pairs(devices, bit))
        low = jnp.where(mine == 0, z, other)
        high = jnp.where(mine == 0, other, z)
        z = jnp.stack([low, high], axis=step)
    return z


def gather_rounds(x, rows, copies):
    sections = rows // copies
    pieces = []
    for t in range(sections):
        pairs = []
        for r in range(rows):
            for c in range(copies):
                q = c * sections + (r + t) % sections
                source = (2 * c + r // sections + t) % copies
                pairs.append((q * copies + source, r * copies + c))
        pieces.append(lax.ppermute(x, AXES, pairs))
    return jnp.stack(pieces)


def local_product(pieces, block_index, block_count, block_values, row_index, copy_index):
    sections = pieces.shape[0]
    block_rows = block_values.shape[2]
    slot_count = block_values.shape[3]
    block_side = block_values.shape[-1]
    width = pieces.shape[-1]
    panels = pieces.reshape(sections * block_rows, block_side, width)
    local = block_index[0, 0] - copy_index * slot_count
    shard = local // block_rows
    arrival = (shard - row_index) % sections
    columns = arrival * block_rows + local % block_rows
    live_slots = jnp.arange(slot_count, dtype=jnp.int32)[None, :] < block_count[0, 0][:, None]
    picked = jnp.take(panels, columns.reshape(-1), axis=0).reshape(
        block_rows, slot_count, block_side, width
    )
    picked = jnp.where(live_slots[:, :, None, None], picked, jnp.zeros((), picked.dtype))
    partial_value = lax.dot_general(
        block_values[0, 0],
        picked,
        (((1, 3), (1, 2)), ((0,), (0,))),
        preferred_element_type=jnp.float32,
    )
    return partial_value.reshape(block_rows * block_side, width)


def shards(features, cotangent, weight_one, weight_two, block_index, block_count, block_values):
    rows = lax.axis_size("row")
    copies = lax.axis_size("rep")
    row_index = lax.axis_index("row")
    copy_index = lax.axis_index("rep")
    devices = rows * copies
    me = row_index * copies + copy_index
    node_rows, feature_width = features.shape
    share_rows = node_rows // copies
    rep_levels = copies.bit_length() - 1
    rep_bits = list(range(rep_levels))
    all_bits = list(range(devices.bit_length() - 1))

    def reduce_rep(partial_value):
        y = partial_value.reshape([2] * rep_levels + [share_rows, partial_value.shape[-1]])
        return reduce_scatter_bits(y, me, rep_bits, devices)

    def gather_rep(z):
        return all_gather_bits(z, me, rep_bits, devices).reshape(node_rows, z.shape[-1])

    stage_in = jnp.concatenate([features, cotangent], axis=1)
    pieces = gather_rounds(stage_in, rows, copies)
    both = reduce_rep(
        local_product(pieces, block_index, block_count, block_values, row_index, copy_index)
    )
    agg_one = both[:, :feature_width].astype(jnp.bfloat16)
    spread_cotangent = both[:, feature_width:]
    carried = lax.dot_general(
        spread_cotangent,
        weight_two.astype(jnp.float32),
        (((1,), (1,)), ((), ())),
        precision=lax.Precision.HIGHEST,
        preferred_element_type=jnp.float32,
    )
    pre_one = jnp.dot(agg_one, weight_one, preferred_element_type=jnp.float32)
    hidden = jax.nn.silu(pre_one).astype(jnp.bfloat16)
    gate_value = jax.nn.sigmoid(pre_one)
    pre_grad = (carried * (gate_value + pre_one * gate_value * (1.0 - gate_value))).astype(
        jnp.bfloat16
    )
    grad_one = lax.dot_general(
        agg_one, pre_grad, (((0,), (0,)), ((), ())), preferred_element_type=jnp.float32
    )
    grad_two = lax.dot_general(
        hidden.astype(jnp.float32),
        spread_cotangent,
        (((0,), (0,)), ((), ())),
        precision=lax.Precision.HIGHEST,
        preferred_element_type=jnp.float32,
    )
    hidden_full = gather_rep(hidden)
    grads = jnp.concatenate([grad_one, grad_two], axis=0)
    grad_rows = grads.shape[0] // copies
    quarter = reduce_scatter_bits(
        grads.reshape([2] * rep_levels + [grad_rows, feature_width]), me, rep_bits, devices
    )
    if grad_rows % rows == 0:
        parts = quarter.reshape(rows, grad_rows // rows, feature_width)
    else:
        parts = quarter.reshape(rows, -1)
    mine = lax.all_to_all(parts, "row", 0, 0, tiled=False).sum(axis=0)
    hidden_full, mine = lax.optimization_barrier((hidden_full, mine))
    pieces_two = gather_rounds(hidden_full, rows, copies)
    spread = lax.all_to_all(jnp.broadcast_to(mine, parts.shape), "row", 0, 0, tiled=False)
    quarter = spread.reshape(grad_rows, feature_width)
    grads = all_gather_bits(quarter, me, rep_bits, devices).reshape(grads.shape)

    agg_two = reduce_rep(
        local_product(pieces_two, block_index, block_count, block_values, row_index, copy_index)
    ).astype(jnp.bfloat16)
    logits = jnp.dot(agg_two, weight_two, preferred_element_type=jnp.float32).astype(jnp.bfloat16)
    return (logits, grads[:feature_width], grads[feature_width:])


def solution(mesh):
    rows = mesh.shape["row"]
    copies = mesh.shape["rep"]
    if not (is_pow2(rows) and is_pow2(copies) and rows % copies == 0):
        raise ValueError("unsupported mesh")
    in_specs = (
        P("row", None),
        P("row", None),
        P(),
        P(),
        P("row", "rep", None, None),
        P("row", "rep", None),
        P("row", "rep", None, None, None, None),
    )
    out_specs = (P(("row", "rep"), None), P(), P())
    return jax.shard_map(shards, mesh=mesh, in_specs=in_specs, out_specs=out_specs, check_vma=False)
```

```python
import jax
import jax.numpy as jnp
from jax import lax
from jax.sharding import PartitionSpec as P

AXES = ("row", "rep")


def is_pow2(n):
    return n > 0 and (n & (n - 1)) == 0


def bit_pairs(devices, bit):
    return [(d, d ^ (1 << bit)) for d in range(devices)]


def reduce_scatter_bits(y, me, bits, devices):
    for step, bit in enumerate(bits):
        axis = len(bits) - 1 - step
        mine = (me >> bit) & 1
        keep = lax.dynamic_index_in_dim(y, mine, axis, keepdims=False)
        send = lax.dynamic_index_in_dim(y, 1 - mine, axis, keepdims=False)
        y = keep + lax.ppermute(send, AXES, bit_pairs(devices, bit))
    return y


def all_gather_bits(z, me, bits, devices):
    for step, bit in enumerate(reversed(bits)):
        mine = (me >> bit) & 1
        other = lax.ppermute(z, AXES, bit_pairs(devices, bit))
        low = jnp.where(mine == 0, z, other)
        high = jnp.where(mine == 0, other, z)
        z = jnp.stack([low, high], axis=step)
    return z


def gather_rounds(x, rows, copies):
    sections = rows // copies
    pieces = []
    for t in range(sections):
        pairs = []
        for r in range(rows):
            for c in range(copies):
                q = c * sections + (r + t) % sections
                source = (2 * c + r // sections + t) % copies
                pairs.append((q * copies + source, r * copies + c))
        pieces.append(lax.ppermute(x, AXES, pairs))
    return jnp.stack(pieces)


def local_product(pieces, block_index, block_count, block_values, row_index, copy_index):
    sections = pieces.shape[0]
    block_rows = block_values.shape[2]
    slot_count = block_values.shape[3]
    block_side = block_values.shape[-1]
    width = pieces.shape[-1]
    panels = pieces.reshape(sections * block_rows, block_side, width)
    local = block_index[0, 0] - copy_index * slot_count
    shard = local // block_rows
    arrival = (shard - row_index) % sections
    columns = arrival * block_rows + local % block_rows
    live_slots = jnp.arange(slot_count, dtype=jnp.int32)[None, :] < block_count[0, 0][:, None]
    picked = jnp.take(panels, columns.reshape(-1), axis=0).reshape(
        block_rows, slot_count, block_side, width
    )
    picked = jnp.where(live_slots[:, :, None, None], picked, jnp.zeros((), picked.dtype))
    partial_value = lax.dot_general(
        block_values[0, 0],
        picked,
        (((1, 3), (1, 2)), ((0,), (0,))),
        preferred_element_type=jnp.float32,
    )
    return partial_value.reshape(block_rows * block_side, width)


def shards(features, cotangent, weight_one, weight_two, block_index, block_count, block_values):
    rows = lax.axis_size("row")
    copies = lax.axis_size("rep")
    row_index = lax.axis_index("row")
    copy_index = lax.axis_index("rep")
    devices = rows * copies
    me = row_index * copies + copy_index
    node_rows, feature_width = features.shape
    share_rows = node_rows // copies
    rep_levels = copies.bit_length() - 1
    rep_bits = list(range(rep_levels))
    all_bits = list(range(devices.bit_length() - 1))

    def reduce_rep(partial_value):
        y = partial_value.reshape([2] * rep_levels + [share_rows, partial_value.shape[-1]])
        return reduce_scatter_bits(y, me, rep_bits, devices)

    def gather_rep(z):
        return all_gather_bits(z, me, rep_bits, devices).reshape(node_rows, z.shape[-1])

    stage_in = jnp.concatenate([features, cotangent], axis=1)
    pieces = gather_rounds(stage_in, rows, copies)
    both = reduce_rep(
        local_product(pieces, block_index, block_count, block_values, row_index, copy_index)
    )
    agg_one = both[:, :feature_width].astype(jnp.bfloat16)
    spread_cotangent = both[:, feature_width:]
    carried = lax.dot_general(
        spread_cotangent,
        weight_two.astype(jnp.float32),
        (((1,), (1,)), ((), ())),
        precision=lax.Precision.HIGHEST,
        preferred_element_type=jnp.float32,
    )
    pre_one = jnp.dot(agg_one, weight_one, preferred_element_type=jnp.float32)
    hidden = jax.nn.silu(pre_one).astype(jnp.bfloat16)
    gate_value = jax.nn.sigmoid(pre_one)
    pre_grad = (carried * (gate_value + pre_one * gate_value * (1.0 - gate_value))).astype(
        jnp.bfloat16
    )
    grad_one = lax.dot_general(
        agg_one, pre_grad, (((0,), (0,)), ((), ())), preferred_element_type=jnp.float32
    )
    grad_two = lax.dot_general(
        hidden.astype(jnp.float32),
        spread_cotangent,
        (((0,), (0,)), ((), ())),
        precision=lax.Precision.HIGHEST,
        preferred_element_type=jnp.float32,
    )
    grads = jnp.concatenate([grad_one, grad_two], axis=0)
    grad_rows = grads.shape[0] // copies
    quarter = reduce_scatter_bits(
        grads.reshape([2] * rep_levels + [grad_rows, feature_width]), me, rep_bits, devices
    )
    hidden, quarter = lax.optimization_barrier((hidden, quarter))
    hidden_full = gather_rep(hidden)
    if grad_rows % rows == 0:
        parts = quarter.reshape(rows, grad_rows // rows, feature_width)
    else:
        parts = quarter.reshape(rows, -1)
    mine = lax.all_to_all(parts, "row", 0, 0, tiled=False).sum(axis=0)
    hidden_full, mine = lax.optimization_barrier((hidden_full, mine))
    pieces_two = gather_rounds(hidden_full, rows, copies)
    spread = lax.all_to_all(jnp.broadcast_to(mine, parts.shape), "row", 0, 0, tiled=False)
    quarter = spread.reshape(grad_rows, feature_width)
    grads = all_gather_bits(quarter, me, rep_bits, devices).reshape(grads.shape)

    agg_two = reduce_rep(
        local_product(pieces_two, block_index, block_count, block_values, row_index, copy_index)
    ).astype(jnp.bfloat16)
    logits = jnp.dot(agg_two, weight_two, preferred_element_type=jnp.float32).astype(jnp.bfloat16)
    return (logits, grads[:feature_width], grads[feature_width:])


def solution(mesh):
    rows = mesh.shape["row"]
    copies = mesh.shape["rep"]
    if not (is_pow2(rows) and is_pow2(copies) and rows % copies == 0):
        raise ValueError("unsupported mesh")
    in_specs = (
        P("row", None),
        P("row", None),
        P(),
        P(),
        P("row", "rep", None, None),
        P("row", "rep", None),
        P("row", "rep", None, None, None, None),
    )
    out_specs = (P(("row", "rep"), None), P(), P())
    return jax.shard_map(shards, mesh=mesh, in_specs=in_specs, out_specs=out_specs, check_vma=False)
```

```python
import jax
import jax.numpy as jnp
from jax import lax
from jax.sharding import PartitionSpec as P

AXES = ("row", "rep")


def is_pow2(n):
    return n > 0 and (n & (n - 1)) == 0


def bit_pairs(devices, bit):
    return [(d, d ^ (1 << bit)) for d in range(devices)]


def reduce_scatter_bits(y, me, bits, devices):
    for step, bit in enumerate(bits):
        axis = len(bits) - 1 - step
        mine = (me >> bit) & 1
        keep = lax.dynamic_index_in_dim(y, mine, axis, keepdims=False)
        send = lax.dynamic_index_in_dim(y, 1 - mine, axis, keepdims=False)
        y = keep + lax.ppermute(send, AXES, bit_pairs(devices, bit))
    return y


def all_gather_bits(z, me, bits, devices):
    for step, bit in enumerate(reversed(bits)):
        mine = (me >> bit) & 1
        other = lax.ppermute(z, AXES, bit_pairs(devices, bit))
        low = jnp.where(mine == 0, z, other)
        high = jnp.where(mine == 0, other, z)
        z = jnp.stack([low, high], axis=step)
    return z


def gather_rounds(x, rows, copies):
    sections = rows // copies
    pieces = []
    for t in range(sections):
        pairs = []
        for r in range(rows):
            for c in range(copies):
                q = c * sections + (r + t) % sections
                source = (2 * c + r // sections + t) % copies
                pairs.append((q * copies + source, r * copies + c))
        pieces.append(lax.ppermute(x, AXES, pairs))
    return jnp.stack(pieces)


def local_product(pieces, block_index, block_count, block_values, row_index, copy_index):
    sections = pieces.shape[0]
    block_rows = block_values.shape[2]
    slot_count = block_values.shape[3]
    block_side = block_values.shape[-1]
    width = pieces.shape[-1]
    panels = pieces.reshape(sections * block_rows, block_side, width)
    local = block_index[0, 0] - copy_index * slot_count
    shard = local // block_rows
    arrival = (shard - row_index) % sections
    columns = arrival * block_rows + local % block_rows
    live_slots = jnp.arange(slot_count, dtype=jnp.int32)[None, :] < block_count[0, 0][:, None]
    picked = jnp.take(panels, columns.reshape(-1), axis=0).reshape(
        block_rows, slot_count, block_side, width
    )
    picked = jnp.where(live_slots[:, :, None, None], picked, jnp.zeros((), picked.dtype))
    partial_value = lax.dot_general(
        block_values[0, 0],
        picked,
        (((1, 3), (1, 2)), ((0,), (0,))),
        preferred_element_type=jnp.float32,
    )
    return partial_value.reshape(block_rows * block_side, width)


def shards(features, cotangent, weight_one, weight_two, block_index, block_count, block_values):
    rows = lax.axis_size("row")
    copies = lax.axis_size("rep")
    row_index = lax.axis_index("row")
    copy_index = lax.axis_index("rep")
    devices = rows * copies
    me = row_index * copies + copy_index
    node_rows, feature_width = features.shape
    share_rows = node_rows // copies
    rep_levels = copies.bit_length() - 1
    rep_bits = list(range(rep_levels))
    all_bits = list(range(devices.bit_length() - 1))

    def reduce_rep(partial_value):
        y = partial_value.reshape([2] * rep_levels + [share_rows, partial_value.shape[-1]])
        return reduce_scatter_bits(y, me, rep_bits, devices)

    def gather_rep(z):
        return all_gather_bits(z, me, rep_bits, devices).reshape(node_rows, z.shape[-1])

    feature_pieces = gather_rounds(features, rows, copies)
    feature_pieces, cotangent_in = lax.optimization_barrier((feature_pieces, cotangent))
    cotangent_pieces = gather_rounds(cotangent_in, rows, copies)
    agg_sum = local_product(
        feature_pieces, block_index, block_count, block_values, row_index, copy_index
    )
    for bit in rep_bits:
        agg_sum = agg_sum + lax.ppermute(agg_sum, AXES, bit_pairs(devices, bit))
    agg_one = agg_sum.astype(jnp.bfloat16)
    pre_one = jnp.dot(agg_one, weight_one, preferred_element_type=jnp.float32)
    hidden = jax.nn.silu(pre_one).astype(jnp.bfloat16)
    gate_value = jax.nn.sigmoid(pre_one)
    slope = gate_value + pre_one * gate_value * (1.0 - gate_value)
    spread_share = local_product(
        cotangent_pieces, block_index, block_count, block_values, row_index, copy_index
    )
    carried_share = lax.dot_general(
        spread_share,
        weight_two.astype(jnp.float32),
        (((1,), (1,)), ((), ())),
        precision=lax.Precision.HIGHEST,
        preferred_element_type=jnp.float32,
    )
    pre_grad_share = carried_share * slope
    grad_one = lax.dot_general(
        agg_one.astype(jnp.float32),
        pre_grad_share,
        (((0,), (0,)), ((), ())),
        precision=lax.Precision.HIGHEST,
        preferred_element_type=jnp.float32,
    )
    grad_two = lax.dot_general(
        hidden.astype(jnp.float32),
        spread_share,
        (((0,), (0,)), ((), ())),
        precision=lax.Precision.HIGHEST,
        preferred_element_type=jnp.float32,
    )
    hidden_full = hidden
    grads = jnp.concatenate([grad_one, grad_two], axis=0)
    grad_rows = grads.shape[0] // copies
    quarter = reduce_scatter_bits(
        grads.reshape([2] * rep_levels + [grad_rows, feature_width]), me, rep_bits, devices
    )
    if grad_rows % rows == 0:
        parts = quarter.reshape(rows, grad_rows // rows, feature_width)
    else:
        parts = quarter.reshape(rows, -1)
    mine = lax.all_to_all(parts, "row", 0, 0, tiled=False).sum(axis=0)
    hidden_full, mine = lax.optimization_barrier((hidden_full, mine))
    pieces_two = gather_rounds(hidden_full, rows, copies)
    spread = lax.all_to_all(jnp.broadcast_to(mine, parts.shape), "row", 0, 0, tiled=False)
    quarter = spread.reshape(grad_rows, feature_width)
    grads = all_gather_bits(quarter, me, rep_bits, devices).reshape(grads.shape)

    agg_two = reduce_rep(
        local_product(pieces_two, block_index, block_count, block_values, row_index, copy_index)
    ).astype(jnp.bfloat16)
    logits = jnp.dot(agg_two, weight_two, preferred_element_type=jnp.float32).astype(jnp.bfloat16)
    return (logits, grads[:feature_width], grads[feature_width:])


def solution(mesh):
    rows = mesh.shape["row"]
    copies = mesh.shape["rep"]
    if not (is_pow2(rows) and is_pow2(copies) and rows % copies == 0):
        raise ValueError("unsupported mesh")
    in_specs = (
        P("row", None),
        P("row", None),
        P(),
        P(),
        P("row", "rep", None, None),
        P("row", "rep", None),
        P("row", "rep", None, None, None, None),
    )
    out_specs = (P(("row", "rep"), None), P(), P())
    return jax.shard_map(shards, mesh=mesh, in_specs=in_specs, out_specs=out_specs, check_vma=False)
```

```python
import jax
import jax.numpy as jnp
from jax import lax
from jax.sharding import PartitionSpec as P

AXES = ("row", "rep")


def is_pow2(n):
    return n > 0 and (n & (n - 1)) == 0


def bit_pairs(devices, bit):
    return [(d, d ^ (1 << bit)) for d in range(devices)]


def reduce_scatter_bits(y, me, bits, devices):
    for step, bit in enumerate(bits):
        axis = len(bits) - 1 - step
        mine = (me >> bit) & 1
        keep = lax.dynamic_index_in_dim(y, mine, axis, keepdims=False)
        send = lax.dynamic_index_in_dim(y, 1 - mine, axis, keepdims=False)
        y = keep + lax.ppermute(send, AXES, bit_pairs(devices, bit))
    return y


def all_gather_bits(z, me, bits, devices):
    for step, bit in enumerate(reversed(bits)):
        mine = (me >> bit) & 1
        other = lax.ppermute(z, AXES, bit_pairs(devices, bit))
        low = jnp.where(mine == 0, z, other)
        high = jnp.where(mine == 0, other, z)
        z = jnp.stack([low, high], axis=step)
    return z


def gather_rounds(x, rows, copies):
    sections = rows // copies
    pieces = []
    for t in range(sections):
        pairs = []
        for r in range(rows):
            for c in range(copies):
                q = c * sections + (r + t) % sections
                source = (2 * c + r // sections + t) % copies
                pairs.append((q * copies + source, r * copies + c))
        pieces.append(lax.ppermute(x, AXES, pairs))
    return jnp.stack(pieces)


def local_product(pieces, block_index, block_count, block_values, row_index, copy_index):
    sections = pieces.shape[0]
    block_rows = block_values.shape[2]
    slot_count = block_values.shape[3]
    block_side = block_values.shape[-1]
    width = pieces.shape[-1]
    panels = pieces.reshape(sections * block_rows, block_side, width)
    local = block_index[0, 0] - copy_index * slot_count
    shard = local // block_rows
    arrival = (shard - row_index) % sections
    columns = arrival * block_rows + local % block_rows
    live_slots = jnp.arange(slot_count, dtype=jnp.int32)[None, :] < block_count[0, 0][:, None]
    picked = jnp.take(panels, columns.reshape(-1), axis=0).reshape(
        block_rows, slot_count, block_side, width
    )
    picked = jnp.where(live_slots[:, :, None, None], picked, jnp.zeros((), picked.dtype))
    partial_value = lax.dot_general(
        block_values[0, 0],
        picked,
        (((1, 3), (1, 2)), ((0,), (0,))),
        preferred_element_type=jnp.float32,
    )
    return partial_value.reshape(block_rows * block_side, width)


def shards(features, cotangent, weight_one, weight_two, block_index, block_count, block_values):
    rows = lax.axis_size("row")
    copies = lax.axis_size("rep")
    row_index = lax.axis_index("row")
    copy_index = lax.axis_index("rep")
    devices = rows * copies
    me = row_index * copies + copy_index
    node_rows, feature_width = features.shape
    share_rows = node_rows // copies
    rep_levels = copies.bit_length() - 1
    rep_bits = list(range(rep_levels))
    all_bits = list(range(devices.bit_length() - 1))

    def reduce_rep(partial_value):
        y = partial_value.reshape([2] * rep_levels + [share_rows, partial_value.shape[-1]])
        return reduce_scatter_bits(y, me, rep_bits, devices)

    def gather_rep(z):
        return all_gather_bits(z, me, rep_bits, devices).reshape(node_rows, z.shape[-1])

    feature_pieces = gather_rounds(features, rows, copies)
    agg_sum = local_product(
        feature_pieces, block_index, block_count, block_values, row_index, copy_index
    )
    for step, bit in enumerate(rep_bits):
        agg_sum = agg_sum + lax.ppermute(agg_sum, AXES, bit_pairs(devices, bit))
        if step == 0:
            agg_sum, cotangent_in, late_values = lax.optimization_barrier(
                (agg_sum, cotangent, block_values)
            )
            cotangent_pieces = gather_rounds(cotangent_in, rows, copies)
    agg_one = agg_sum.astype(jnp.bfloat16)
    pre_one = jnp.dot(agg_one, weight_one, preferred_element_type=jnp.float32)
    hidden = jax.nn.silu(pre_one).astype(jnp.bfloat16)
    gate_value = jax.nn.sigmoid(pre_one)
    slope = gate_value + pre_one * gate_value * (1.0 - gate_value)
    spread_share = local_product(
        cotangent_pieces, block_index, block_count, late_values, row_index, copy_index
    )
    carried_share = lax.dot_general(
        spread_share,
        weight_two.astype(jnp.float32),
        (((1,), (1,)), ((), ())),
        precision=lax.Precision.HIGHEST,
        preferred_element_type=jnp.float32,
    )
    pre_grad_share = carried_share * slope
    grad_one = lax.dot_general(
        agg_one.astype(jnp.float32),
        pre_grad_share,
        (((0,), (0,)), ((), ())),
        precision=lax.Precision.HIGHEST,
        preferred_element_type=jnp.float32,
    )
    grad_two = lax.dot_general(
        hidden.astype(jnp.float32),
        spread_share,
        (((0,), (0,)), ((), ())),
        precision=lax.Precision.HIGHEST,
        preferred_element_type=jnp.float32,
    )
    hidden_full = hidden
    grads = jnp.concatenate([grad_one, grad_two], axis=0)
    grad_rows = grads.shape[0] // copies
    quarter = reduce_scatter_bits(
        grads.reshape([2] * rep_levels + [grad_rows, feature_width]), me, rep_bits, devices
    )
    if grad_rows % rows == 0:
        parts = quarter.reshape(rows, grad_rows // rows, feature_width)
    else:
        parts = quarter.reshape(rows, -1)
    mine = lax.all_to_all(parts, "row", 0, 0, tiled=False).sum(axis=0)
    hidden_full, mine = lax.optimization_barrier((hidden_full, mine))
    pieces_two = gather_rounds(hidden_full, rows, copies)
    spread = lax.all_to_all(jnp.broadcast_to(mine, parts.shape), "row", 0, 0, tiled=False)
    quarter = spread.reshape(grad_rows, feature_width)
    grads = all_gather_bits(quarter, me, rep_bits, devices).reshape(grads.shape)

    agg_two = reduce_rep(
        local_product(pieces_two, block_index, block_count, block_values, row_index, copy_index)
    ).astype(jnp.bfloat16)
    logits = jnp.dot(agg_two, weight_two, preferred_element_type=jnp.float32).astype(jnp.bfloat16)
    return (logits, grads[:feature_width], grads[feature_width:])


def solution(mesh):
    rows = mesh.shape["row"]
    copies = mesh.shape["rep"]
    if not (is_pow2(rows) and is_pow2(copies) and rows % copies == 0):
        raise ValueError("unsupported mesh")
    in_specs = (
        P("row", None),
        P("row", None),
        P(),
        P(),
        P("row", "rep", None, None),
        P("row", "rep", None),
        P("row", "rep", None, None, None, None),
    )
    out_specs = (P(("row", "rep"), None), P(), P())
    return jax.shard_map(shards, mesh=mesh, in_specs=in_specs, out_specs=out_specs, check_vma=False)
```

```python
import jax
import jax.numpy as jnp
from jax import lax
from jax.sharding import PartitionSpec as P

AXES = ("row", "rep")


def is_pow2(n):
    return n > 0 and (n & (n - 1)) == 0


def bit_pairs(devices, bit):
    return [(d, d ^ (1 << bit)) for d in range(devices)]


def reduce_scatter_bits(y, me, bits, devices):
    for step, bit in enumerate(bits):
        axis = len(bits) - 1 - step
        mine = (me >> bit) & 1
        keep = lax.dynamic_index_in_dim(y, mine, axis, keepdims=False)
        send = lax.dynamic_index_in_dim(y, 1 - mine, axis, keepdims=False)
        y = keep + lax.ppermute(send, AXES, bit_pairs(devices, bit))
    return y


def all_gather_bits(z, me, bits, devices):
    for step, bit in enumerate(reversed(bits)):
        mine = (me >> bit) & 1
        other = lax.ppermute(z, AXES, bit_pairs(devices, bit))
        low = jnp.where(mine == 0, z, other)
        high = jnp.where(mine == 0, other, z)
        z = jnp.stack([low, high], axis=step)
    return z


def gather_rounds(x, rows, copies):
    sections = rows // copies
    pieces = []
    for t in range(sections):
        pairs = []
        for r in range(rows):
            for c in range(copies):
                q = c * sections + (r + t) % sections
                source = (2 * c + r // sections + t) % copies
                pairs.append((q * copies + source, r * copies + c))
        pieces.append(lax.ppermute(x, AXES, pairs))
    return jnp.stack(pieces)


def local_product(pieces, block_index, block_count, block_values, row_index, copy_index):
    sections = pieces.shape[0]
    block_rows = block_values.shape[2]
    slot_count = block_values.shape[3]
    block_side = block_values.shape[-1]
    width = pieces.shape[-1]
    panels = pieces.reshape(sections * block_rows, block_side, width)
    local = block_index[0, 0] - copy_index * slot_count
    shard = local // block_rows
    arrival = (shard - row_index) % sections
    columns = arrival * block_rows + local % block_rows
    live_slots = jnp.arange(slot_count, dtype=jnp.int32)[None, :] < block_count[0, 0][:, None]
    picked = jnp.take(panels, columns.reshape(-1), axis=0).reshape(
        block_rows, slot_count, block_side, width
    )
    picked = jnp.where(live_slots[:, :, None, None], picked, jnp.zeros((), picked.dtype))
    partial_value = lax.dot_general(
        block_values[0, 0],
        picked,
        (((1, 3), (1, 2)), ((0,), (0,))),
        preferred_element_type=jnp.float32,
    )
    return partial_value.reshape(block_rows * block_side, width)


def shards(features, cotangent, weight_one, weight_two, block_index, block_count, block_values):
    rows = lax.axis_size("row")
    copies = lax.axis_size("rep")
    row_index = lax.axis_index("row")
    copy_index = lax.axis_index("rep")
    devices = rows * copies
    me = row_index * copies + copy_index
    node_rows, feature_width = features.shape
    share_rows = node_rows // copies
    rep_levels = copies.bit_length() - 1
    rep_bits = list(range(rep_levels))
    all_bits = list(range(devices.bit_length() - 1))

    def reduce_rep(partial_value):
        y = partial_value.reshape([2] * rep_levels + [share_rows, partial_value.shape[-1]])
        return reduce_scatter_bits(y, me, rep_bits, devices)

    def gather_rep(z):
        return all_gather_bits(z, me, rep_bits, devices).reshape(node_rows, z.shape[-1])

    feature_pieces = gather_rounds(features, rows, copies)
    agg_sum = local_product(
        feature_pieces, block_index, block_count, block_values, row_index, copy_index
    )
    agg_sum = agg_sum.reshape([2] * rep_levels + [share_rows, feature_width])
    for step, bit in enumerate(rep_bits):
        axis = rep_levels - 1 - step
        mine = (me >> bit) & 1
        keep = lax.dynamic_index_in_dim(agg_sum, mine, axis, keepdims=False)
        send = lax.dynamic_index_in_dim(agg_sum, 1 - mine, axis, keepdims=False)
        agg_sum = keep + lax.ppermute(send, AXES, bit_pairs(devices, bit))
        if step == 0:
            agg_sum, cotangent_in, late_values = lax.optimization_barrier(
                (agg_sum, cotangent, block_values)
            )
            cotangent_pieces = gather_rounds(cotangent_in, rows, copies)
    agg_one = gather_rep(agg_sum.astype(jnp.bfloat16))
    pre_one = jnp.dot(agg_one, weight_one, preferred_element_type=jnp.float32)
    hidden = jax.nn.silu(pre_one).astype(jnp.bfloat16)
    gate_value = jax.nn.sigmoid(pre_one)
    slope = gate_value + pre_one * gate_value * (1.0 - gate_value)
    spread_share = local_product(
        cotangent_pieces, block_index, block_count, late_values, row_index, copy_index
    )
    carried_share = lax.dot_general(
        spread_share,
        weight_two.astype(jnp.float32),
        (((1,), (1,)), ((), ())),
        precision=lax.Precision.HIGHEST,
        preferred_element_type=jnp.float32,
    )
    pre_grad_share = carried_share * slope
    grad_one = lax.dot_general(
        agg_one.astype(jnp.float32),
        pre_grad_share,
        (((0,), (0,)), ((), ())),
        precision=lax.Precision.HIGHEST,
        preferred_element_type=jnp.float32,
    )
    grad_two = lax.dot_general(
        hidden.astype(jnp.float32),
        spread_share,
        (((0,), (0,)), ((), ())),
        precision=lax.Precision.HIGHEST,
        preferred_element_type=jnp.float32,
    )
    hidden_full = hidden
    grads = jnp.concatenate([grad_one, grad_two], axis=0)
    grad_rows = grads.shape[0] // copies
    quarter = reduce_scatter_bits(
        grads.reshape([2] * rep_levels + [grad_rows, feature_width]), me, rep_bits, devices
    )
    if grad_rows % rows == 0:
        parts = quarter.reshape(rows, grad_rows // rows, feature_width)
    else:
        parts = quarter.reshape(rows, -1)
    mine = lax.all_to_all(parts, "row", 0, 0, tiled=False).sum(axis=0)
    hidden_full, mine = lax.optimization_barrier((hidden_full, mine))
    pieces_two = gather_rounds(hidden_full, rows, copies)
    spread = lax.all_to_all(jnp.broadcast_to(mine, parts.shape), "row", 0, 0, tiled=False)
    quarter = spread.reshape(grad_rows, feature_width)
    grads = all_gather_bits(quarter, me, rep_bits, devices).reshape(grads.shape)

    agg_two = reduce_rep(
        local_product(pieces_two, block_index, block_count, block_values, row_index, copy_index)
    ).astype(jnp.bfloat16)
    logits = jnp.dot(agg_two, weight_two, preferred_element_type=jnp.float32).astype(jnp.bfloat16)
    return (logits, grads[:feature_width], grads[feature_width:])


def solution(mesh):
    rows = mesh.shape["row"]
    copies = mesh.shape["rep"]
    if not (is_pow2(rows) and is_pow2(copies) and rows % copies == 0):
        raise ValueError("unsupported mesh")
    in_specs = (
        P("row", None),
        P("row", None),
        P(),
        P(),
        P("row", "rep", None, None),
        P("row", "rep", None),
        P("row", "rep", None, None, None, None),
    )
    out_specs = (P(("row", "rep"), None), P(), P())
    return jax.shard_map(shards, mesh=mesh, in_specs=in_specs, out_specs=out_specs, check_vma=False)
```

```python
import jax
import jax.numpy as jnp
from jax import lax
from jax.sharding import PartitionSpec as P

AXES = ("row", "rep")


def is_pow2(n):
    return n > 0 and (n & (n - 1)) == 0


def bit_pairs(devices, bit):
    return [(d, d ^ (1 << bit)) for d in range(devices)]


def reduce_scatter_bits(y, me, bits, devices):
    for step, bit in enumerate(bits):
        axis = len(bits) - 1 - step
        mine = (me >> bit) & 1
        keep = lax.dynamic_index_in_dim(y, mine, axis, keepdims=False)
        send = lax.dynamic_index_in_dim(y, 1 - mine, axis, keepdims=False)
        y = keep + lax.ppermute(send, AXES, bit_pairs(devices, bit))
    return y


def all_gather_bits(z, me, bits, devices):
    for step, bit in enumerate(reversed(bits)):
        mine = (me >> bit) & 1
        other = lax.ppermute(z, AXES, bit_pairs(devices, bit))
        low = jnp.where(mine == 0, z, other)
        high = jnp.where(mine == 0, other, z)
        z = jnp.stack([low, high], axis=step)
    return z


def gather_rounds(x, rows, copies):
    sections = rows // copies
    pieces = []
    for t in range(sections):
        pairs = []
        for r in range(rows):
            for c in range(copies):
                q = c * sections + (r + t) % sections
                source = (2 * c + r // sections + t) % copies
                pairs.append((q * copies + source, r * copies + c))
        pieces.append(lax.ppermute(x, AXES, pairs))
    return jnp.stack(pieces)


def local_product(pieces, block_index, block_count, block_values, row_index, copy_index):
    sections = pieces.shape[0]
    block_rows = block_values.shape[2]
    slot_count = block_values.shape[3]
    block_side = block_values.shape[-1]
    width = pieces.shape[-1]
    panels = pieces.reshape(sections * block_rows, block_side, width)
    local = block_index[0, 0] - copy_index * slot_count
    shard = local // block_rows
    arrival = (shard - row_index) % sections
    columns = arrival * block_rows + local % block_rows
    live_slots = jnp.arange(slot_count, dtype=jnp.int32)[None, :] < block_count[0, 0][:, None]
    picked = jnp.take(panels, columns.reshape(-1), axis=0).reshape(
        block_rows, slot_count, block_side, width
    )
    picked = jnp.where(live_slots[:, :, None, None], picked, jnp.zeros((), picked.dtype))
    partial_value = lax.dot_general(
        block_values[0, 0],
        picked,
        (((1, 3), (1, 2)), ((0,), (0,))),
        preferred_element_type=jnp.float32,
    )
    return partial_value.reshape(block_rows * block_side, width)


def shards(features, cotangent, weight_one, weight_two, block_index, block_count, block_values):
    rows = lax.axis_size("row")
    copies = lax.axis_size("rep")
    row_index = lax.axis_index("row")
    copy_index = lax.axis_index("rep")
    devices = rows * copies
    me = row_index * copies + copy_index
    node_rows, feature_width = features.shape
    share_rows = node_rows // copies
    rep_levels = copies.bit_length() - 1
    rep_bits = list(range(rep_levels))
    all_bits = list(range(devices.bit_length() - 1))

    def reduce_rep(partial_value):
        y = partial_value.reshape([2] * rep_levels + [share_rows, partial_value.shape[-1]])
        return reduce_scatter_bits(y, me, rep_bits, devices)

    def gather_rep(z):
        return all_gather_bits(z, me, rep_bits, devices).reshape(node_rows, z.shape[-1])

    stage_in = jnp.concatenate([features, cotangent], axis=1)
    pieces = gather_rounds(stage_in, rows, copies)
    both = reduce_rep(
        local_product(pieces, block_index, block_count, block_values, row_index, copy_index)
    )
    agg_one = both[:, :feature_width].astype(jnp.bfloat16)
    spread_cotangent = both[:, feature_width:]
    carried = lax.dot_general(
        spread_cotangent,
        weight_two.astype(jnp.float32),
        (((1,), (1,)), ((), ())),
        precision=lax.Precision.HIGHEST,
        preferred_element_type=jnp.float32,
    )
    pre_one = jnp.dot(agg_one, weight_one, preferred_element_type=jnp.float32)
    hidden = jax.nn.silu(pre_one).astype(jnp.bfloat16)
    gate_value = jax.nn.sigmoid(pre_one)
    pre_grad = (carried * (gate_value + pre_one * gate_value * (1.0 - gate_value))).astype(
        jnp.bfloat16
    )
    grad_one = lax.dot_general(
        agg_one, pre_grad, (((0,), (0,)), ((), ())), preferred_element_type=jnp.float32
    )
    grad_two = lax.dot_general(
        hidden.astype(jnp.float32),
        spread_cotangent,
        (((0,), (0,)), ((), ())),
        precision=lax.Precision.HIGHEST,
        preferred_element_type=jnp.float32,
    )
    grads = jnp.concatenate([grad_one, grad_two], axis=0)
    grad_rows = grads.shape[0] // copies
    quarter = reduce_scatter_bits(
        grads.reshape([2] * rep_levels + [grad_rows, feature_width]), me, rep_bits, devices
    )
    if grad_rows % rows == 0:
        parts = quarter.reshape(rows, grad_rows // rows, feature_width)
    else:
        parts = quarter.reshape(rows, -1)
    mine = lax.all_to_all(parts, "row", 0, 0, tiled=False).sum(axis=0)
    hidden, mine = lax.optimization_barrier((hidden, mine))
    hidden_full = gather_rep(hidden)
    pieces_two = gather_rounds(hidden_full, rows, copies)
    spread = lax.all_to_all(jnp.broadcast_to(mine, parts.shape), "row", 0, 0, tiled=False)
    quarter = spread.reshape(grad_rows, feature_width)
    grads = all_gather_bits(quarter, me, rep_bits, devices).reshape(grads.shape)

    agg_two = reduce_rep(
        local_product(pieces_two, block_index, block_count, block_values, row_index, copy_index)
    ).astype(jnp.bfloat16)
    logits = jnp.dot(agg_two, weight_two, preferred_element_type=jnp.float32).astype(jnp.bfloat16)
    return (logits, grads[:feature_width], grads[feature_width:])


def solution(mesh):
    rows = mesh.shape["row"]
    copies = mesh.shape["rep"]
    if not (is_pow2(rows) and is_pow2(copies) and rows % copies == 0):
        raise ValueError("unsupported mesh")
    in_specs = (
        P("row", None),
        P("row", None),
        P(),
        P(),
        P("row", "rep", None, None),
        P("row", "rep", None),
        P("row", "rep", None, None, None, None),
    )
    out_specs = (P(("row", "rep"), None), P(), P())
    return jax.shard_map(shards, mesh=mesh, in_specs=in_specs, out_specs=out_specs, check_vma=False)
```

```python
import jax
import jax.numpy as jnp
from jax import lax
from jax.sharding import PartitionSpec as P

AXES = ("row", "rep")


def is_pow2(n):
    return n > 0 and (n & (n - 1)) == 0


def bit_pairs(devices, bit):
    return [(d, d ^ (1 << bit)) for d in range(devices)]


def reduce_scatter_bits(y, me, bits, devices):
    for step, bit in enumerate(bits):
        axis = len(bits) - 1 - step
        mine = (me >> bit) & 1
        keep = lax.dynamic_index_in_dim(y, mine, axis, keepdims=False)
        send = lax.dynamic_index_in_dim(y, 1 - mine, axis, keepdims=False)
        y = keep + lax.ppermute(send, AXES, bit_pairs(devices, bit))
    return y


def all_gather_bits(z, me, bits, devices):
    for step, bit in enumerate(reversed(bits)):
        mine = (me >> bit) & 1
        other = lax.ppermute(z, AXES, bit_pairs(devices, bit))
        low = jnp.where(mine == 0, z, other)
        high = jnp.where(mine == 0, other, z)
        z = jnp.stack([low, high], axis=step)
    return z


def gather_rounds(x, rows, copies):
    sections = rows // copies
    pieces = []
    for t in range(sections):
        pairs = []
        for r in range(rows):
            for c in range(copies):
                q = c * sections + (r + t) % sections
                source = (2 * c + r // sections + t) % copies
                pairs.append((q * copies + source, r * copies + c))
        pieces.append(lax.ppermute(x, AXES, pairs))
    return jnp.stack(pieces)


def panel_blocks(block_index, block_count, block_values, row_index, copy_index, sections):
    block_rows = block_values.shape[2]
    slot_count = block_values.shape[3]
    local = block_index[0, 0] - copy_index * slot_count
    shard = local // block_rows
    arrival = (shard - row_index) % sections
    columns = arrival * block_rows + local % block_rows
    live_slots = jnp.arange(slot_count, dtype=jnp.int32)[None, :] < block_count[0, 0][:, None]
    panel_ids = jnp.arange(sections * block_rows, dtype=jnp.int32)
    onehot = (columns[:, :, None] == panel_ids[None, None, :]) & live_slots[:, :, None]
    placed = jnp.einsum(
        "asp,asxy->axpy",
        onehot.astype(block_values.dtype),
        block_values[0, 0],
        preferred_element_type=jnp.float32,
    )
    return placed.astype(block_values.dtype)


def local_product(pieces, placed):
    sections = pieces.shape[0]
    block_rows, block_side = placed.shape[0], placed.shape[1]
    width = pieces.shape[-1]
    panels = pieces.reshape(sections * block_rows, block_side, width)
    partial_value = lax.dot_general(
        placed, panels, (((2, 3), (0, 1)), ((), ())), preferred_element_type=jnp.float32
    )
    return partial_value.reshape(block_rows * block_side, width)


def shards(features, cotangent, weight_one, weight_two, block_index, block_count, block_values):
    rows = lax.axis_size("row")
    copies = lax.axis_size("rep")
    row_index = lax.axis_index("row")
    copy_index = lax.axis_index("rep")
    devices = rows * copies
    me = row_index * copies + copy_index
    node_rows, feature_width = features.shape
    share_rows = node_rows // copies
    rep_levels = copies.bit_length() - 1
    rep_bits = list(range(rep_levels))
    all_bits = list(range(devices.bit_length() - 1))

    def reduce_rep(partial_value):
        y = partial_value.reshape([2] * rep_levels + [share_rows, partial_value.shape[-1]])
        return reduce_scatter_bits(y, me, rep_bits, devices)

    def gather_rep(z):
        return all_gather_bits(z, me, rep_bits, devices).reshape(node_rows, z.shape[-1])

    placed = panel_blocks(
        block_index, block_count, block_values, row_index, copy_index, rows // copies
    )
    stage_in = jnp.concatenate([features, cotangent], axis=1)
    pieces = gather_rounds(stage_in, rows, copies)
    both = reduce_rep(
        local_product(pieces, placed)
    )
    agg_one = both[:, :feature_width].astype(jnp.bfloat16)
    spread_cotangent = both[:, feature_width:]
    carried = lax.dot_general(
        spread_cotangent,
        weight_two.astype(jnp.float32),
        (((1,), (1,)), ((), ())),
        precision=lax.Precision.HIGHEST,
        preferred_element_type=jnp.float32,
    )
    pre_one = jnp.dot(agg_one, weight_one, preferred_element_type=jnp.float32)
    hidden = jax.nn.silu(pre_one).astype(jnp.bfloat16)
    gate_value = jax.nn.sigmoid(pre_one)
    pre_grad = (carried * (gate_value + pre_one * gate_value * (1.0 - gate_value))).astype(
        jnp.bfloat16
    )
    grad_one = lax.dot_general(
        agg_one, pre_grad, (((0,), (0,)), ((), ())), preferred_element_type=jnp.float32
    )
    grad_two = lax.dot_general(
        hidden.astype(jnp.float32),
        spread_cotangent,
        (((0,), (0,)), ((), ())),
        precision=lax.Precision.HIGHEST,
        preferred_element_type=jnp.float32,
    )
    hidden_full = gather_rep(hidden)
    grads = jnp.concatenate([grad_one, grad_two], axis=0)
    grad_rows = grads.shape[0] // copies
    quarter = reduce_scatter_bits(
        grads.reshape([2] * rep_levels + [grad_rows, feature_width]), me, rep_bits, devices
    )
    if grad_rows % rows == 0:
        parts = quarter.reshape(rows, grad_rows // rows, feature_width)
    else:
        parts = quarter.reshape(rows, -1)
    mine = lax.all_to_all(parts, "row", 0, 0, tiled=False).sum(axis=0)
    hidden_full, mine = lax.optimization_barrier((hidden_full, mine))
    pieces_two = gather_rounds(hidden_full, rows, copies)
    spread = lax.all_to_all(jnp.broadcast_to(mine, parts.shape), "row", 0, 0, tiled=False)
    quarter = spread.reshape(grad_rows, feature_width)
    grads = all_gather_bits(quarter, me, rep_bits, devices).reshape(grads.shape)

    agg_two = reduce_rep(
        local_product(pieces_two, placed)
    ).astype(jnp.bfloat16)
    logits = jnp.dot(agg_two, weight_two, preferred_element_type=jnp.float32).astype(jnp.bfloat16)
    return (logits, grads[:feature_width], grads[feature_width:])


def solution(mesh):
    rows = mesh.shape["row"]
    copies = mesh.shape["rep"]
    if not (is_pow2(rows) and is_pow2(copies) and rows % copies == 0):
        raise ValueError("unsupported mesh")
    in_specs = (
        P("row", None),
        P("row", None),
        P(),
        P(),
        P("row", "rep", None, None),
        P("row", "rep", None),
        P("row", "rep", None, None, None, None),
    )
    out_specs = (P(("row", "rep"), None), P(), P())
    return jax.shard_map(shards, mesh=mesh, in_specs=in_specs, out_specs=out_specs, check_vma=False)
```
